256 devices in a mesh: along: 32 (over y_hi, z, core), across: 8 (over x, y_lo).
Axes of the slice: x: 4, y: 4 (y_hi: 2, y_lo: 2; y = y_hi * 2 + y_lo), z: 8, core: 2. Of those that a mesh axis runs over, the one named last changes fastest.
Arguments:
- disp: float32 [2, 4096, 4096], P(None, 'along', 'across'), may hold values from -0.1 to 0.1
- velocity: float32 [2, 4096, 4096], P(None, 'along', 'across'), may hold values from -6 to 6
- bond_bits: int32 [2, 4096, 4096], P(None, 'along', 'across'), may hold values from 0 to 16383
- panel_pos: float32 [2048, 2], P('along'), as said below
- contact_list: int32 [32, 4], P('along'), may hold values from 0 to 255, as said below
Outputs:
- new_disp: float32 [2, 4096, 4096], P(None, 'along', 'across')
- new_velocity: float32 [2, 4096, 4096], P(None, 'along', 'across')
- damage: float32 [4096, 4096], P('along', 'across')
- panel_force: float32 [2048, 2], P('along')
The draws below stay inside these ranges and needn't reach their ends.
Inputs may be any that keep to these rules, and one draw needn't show every extreme that they name: `contact_list`: each row lists 4 different tiles. `panel_pos`: every panel lies inside some tile of its block's contact list.
All inputs are finite; a program needn't handle non-finite values.
Results may differ from the reference program's by a relative error of at most 0.0003.
Values sent between devices are 32-bit elements; how exact they have to be, the bound alone decides.
No kernel may reach another device: no remote copies, remote signals or barrier semaphores. Data moves between devices by JAX's collectives and lax.ppermute only.
A program may use at most 64 MiB of HBM per device.

```python
import jax
import jax.numpy as jnp
from jax import lax

TA = 128
TC = 512
PAN_DEV = 64
CL = 4
NA = 4096
NC = 4096
NBLK = 32
P_SIZE = 2048
TILES = 256
N_ACROSS = 8


def list_helper(key):
    inner = jax.random.fold_in(key, 11)
    tile_ids = jnp.arange(TILES, dtype=jnp.int32)
    block_ids = jnp.arange(NBLK, dtype=jnp.int32)
    bow = tile_ids // N_ACROSS < 2
    raw = jax.random.randint(inner, (NBLK, TILES), 0, 1 << 20, dtype=jnp.int32)
    score = jnp.where(bow[None, :], raw // 8, raw) * TILES + tile_ids[None, :]
    first_pair = (block_ids[:, None] == 0) & (tile_ids[None, :] == 0)
    last_pair = (block_ids[:, None] == NBLK - 1) & (tile_ids[None, :] == TILES - 1)
    score = jnp.where(first_pair | last_pair, -1, score)
    return jnp.argsort(score, axis=1, stable=True)[:, :CL].astype(jnp.int32)


def draw_contact_list(key, part):
    return list_helper(key)


def draw_panel_pos(key, part):
    lists = list_helper(key)
    slot_key = jax.random.fold_in(key, 23)
    row_key = jax.random.fold_in(key, 29)
    col_key = jax.random.fold_in(key, 31)
    slot = jax.random.randint(slot_key, (P_SIZE,), 0, CL, dtype=jnp.int32)
    block = jnp.arange(P_SIZE, dtype=jnp.int32) // PAN_DEV
    tile = lists[block, slot]
    base_row = (tile // N_ACROSS * TA).astype(jnp.float32)
    base_col = (tile % N_ACROSS * TC).astype(jnp.float32)
    off_row = jax.random.uniform(row_key, (P_SIZE,), jnp.float32, 0.0, float(TA))
    off_col = jax.random.uniform(col_key, (P_SIZE,), jnp.float32, 0.0, float(TC))
    return jnp.stack([base_row + off_row, base_col + off_col], axis=1)


def place_ends(values, key, low, high):
    spot = [jax.random.randint(jax.random.fold_in(key, axis), (), 0, length) for axis, length in enumerate(values.shape)]
    longest = values.shape.index(max(values.shape))
    next_to = spot[:longest] + [(spot[longest] + 1) % values.shape[longest]] + spot[longest + 1:]
    return values.at[tuple(spot)].set(low).at[tuple(next_to)].set(high)


def block_levels(key, dims, cuts, smallest, top_value):
    gain, own = 1.0, jax.random.fold_in(key, 6)
    for position, parts in cuts:
        heights = jnp.exp(jax.random.uniform(jax.random.fold_in(own, position), (parts,), jnp.float32, smallest / len(cuts), top_value / len(cuts)))
        gain = gain * jnp.repeat(heights, dims[position] // parts).reshape([-1 if axis == position else 1 for axis in range(len(dims))])
    return gain


def normal_values(rng, shape, spread, most, cuts=(), held_as=jnp.bfloat16):
    factor_of = block_levels(rng, shape, cuts, -0.22, 0.18) if cuts else 1.0
    result = jax.random.normal(rng, shape, jnp.float32) * spread * factor_of
    return jnp.minimum(jnp.maximum(result, -most), most).astype(held_as)


def setup_inputs(seed: int = 0) -> dict:
    arg_keys = jax.random.split(jax.random.key(seed), 6)
    return {
        "disp": normal_values(arg_keys[0], (2, NA, NC), 0.02, 0.1, ((1, 32), (2, 8)), jnp.float32),
        "velocity": normal_values(arg_keys[1], (2, NA, NC), 1.0, 6.0, ((1, 32), (2, 8)), jnp.float32),
        "bond_bits": place_ends(jax.random.randint(arg_keys[2], (2, NA, NC), 0, 16384), jax.random.fold_in(arg_keys[2], 1), 0, 16383).astype(jnp.int32),
        "panel_pos": draw_panel_pos(jax.random.fold_in(arg_keys[5], 71), 0),
        "contact_list": draw_contact_list(jax.random.fold_in(arg_keys[5], 71), 0),
    }


offsets = [(rr, cc) for rr in range(-3, 4) for cc in range(-3, 4) if 0 < rr * rr + cc * cc <= 9]

def forces(padded, bits, present_pad, rows, cols):
    centre = padded[:, 3:3 + rows, 3:3 + cols]
    total_row = jnp.zeros((rows, cols), jnp.float32)
    total_col = jnp.zeros((rows, cols), jnp.float32)
    kept_sum = jnp.zeros((rows, cols), jnp.float32)
    exist_sum = jnp.zeros((rows, cols), jnp.float32)
    for index, (row_off, col_off) in enumerate(offsets):
        other = padded[:, 3 + row_off:3 + row_off + rows, 3 + col_off:3 + col_off + cols]
        present = present_pad[3 + row_off:3 + row_off + rows, 3 + col_off:3 + col_off + cols]
        flag = jnp.bitwise_and(jnp.right_shift(bits[index // 14], index % 14), 1).astype(jnp.float32)
        keep = flag * present
        row_part = row_off + (other[0] - centre[0])
        col_part = col_off + (other[1] - centre[1])
        length = jnp.sqrt(row_part * row_part + col_part * col_part)
        rest = float((row_off * row_off + col_off * col_off) ** 0.5)
        coeff = keep * (length - rest) / (rest * length)
        total_row = total_row + coeff * row_part
        total_col = total_col + coeff * col_part
        kept_sum = kept_sum + keep
        exist_sum = exist_sum + present
    return (jnp.stack([total_row, total_col]), kept_sum, exist_sum)

def reference(disp, velocity, bond_bits, panel_pos, contact_list):
    present_pad = jnp.pad(jnp.ones((NA, NC), jnp.float32), 3)
    state_u, state_v = (disp, velocity)
    damage = None
    for step in range(2):
        padded = jnp.pad(state_u, ((0, 0), (3, 3), (3, 3)))
        force, kept_sum, exist_sum = forces(padded, bond_bits, present_pad, NA, NC)
        if step == 0:
            damage = 1.0 - kept_sum / exist_sum
        state_v = state_v + 10.0 * force
        state_u = state_u + 0.05 * state_v
    row_pos = jnp.arange(NA, dtype=jnp.int32).astype(jnp.float32)[:, None] + state_u[0]
    col_pos = jnp.arange(NC, dtype=jnp.int32).astype(jnp.float32)[None, :] + state_u[1]

    def per_block(block):
        centres = lax.dynamic_slice_in_dim(panel_pos, (block * PAN_DEV).astype(jnp.int32), PAN_DEV, 0)

        def per_tile(carry, tile):
            tile_row = (tile // N_ACROSS * TA).astype(jnp.int32)
            tile_col = (tile % N_ACROSS * TC).astype(jnp.int32)
            rows_x = lax.dynamic_slice(row_pos, (tile_row, tile_col), (TA, TC)).reshape(-1)
            cols_x = lax.dynamic_slice(col_pos, (tile_row, tile_col), (TA, TC)).reshape(-1)
            delta_row = centres[:, 0:1] - rows_x[None, :]
            delta_col = centres[:, 1:2] - cols_x[None, :]
            push = 0.5 * jnp.maximum(4.0 - delta_row * delta_row - delta_col * delta_col, 0.0)
            part = jnp.stack([lax.optimization_barrier(jnp.sum(push * delta_row, axis=1)), lax.optimization_barrier(jnp.sum(push * delta_col, axis=1))], axis=1)
            return (carry + part, None)
        total, unused = lax.scan(per_tile, jnp.zeros((PAN_DEV, 2), jnp.float32), contact_list[block])
        return total
    panel_force = lax.map(per_block, jnp.arange(NBLK, dtype=jnp.int32)).reshape(P_SIZE, 2)
    return (state_u, state_v, damage, panel_force)
```

```python
import jax
import jax.numpy as jnp
from jax import lax
from jax.sharding import PartitionSpec as P

PAN_DEV = 64


offsets = [(rr, cc) for rr in range(-3, 4) for cc in range(-3, 4) if 0 < rr * rr + cc * cc <= 9]


def with_halo(block, sides, width):
    for axis, dim in sides:
        count = lax.axis_size(axis)
        forward = [(i, i + 1) for i in range(count - 1)]
        backward = [(target, source) for source, target in forward]
        low = lax.ppermute(
            lax.slice_in_dim(block, block.shape[dim] - width, None, axis=dim), axis, forward
        )
        high = lax.ppermute(lax.slice_in_dim(block, 0, width, axis=dim), axis, backward)
        block = jnp.concatenate([low, block, high], axis=dim)
    return block


def forces(padded, bits, present_pad, rows, cols):
    centre = padded[:, 3 : 3 + rows, 3 : 3 + cols]
    total_row = jnp.zeros((rows, cols), jnp.float32)
    total_col = jnp.zeros((rows, cols), jnp.float32)
    kept_sum = jnp.zeros((rows, cols), jnp.float32)
    exist_sum = jnp.zeros((rows, cols), jnp.float32)
    for index, (row_off, col_off) in enumerate(offsets):
        other = padded[:, 3 + row_off : 3 + row_off + rows, 3 + col_off : 3 + col_off + cols]
        present = present_pad[3 + row_off : 3 + row_off + rows, 3 + col_off : 3 + col_off + cols]
        flag = jnp.bitwise_and(jnp.right_shift(bits[index // 14], index % 14), 1).astype(
            jnp.float32
        )
        keep = flag * present
        row_part = row_off + (other[0] - centre[0])
        col_part = col_off + (other[1] - centre[1])
        length = jnp.sqrt(row_part * row_part + col_part * col_part)
        rest = float((row_off * row_off + col_off * col_off) ** 0.5)
        coeff = keep * (length - rest) / (rest * length)
        total_row = total_row + coeff * row_part
        total_col = total_col + coeff * col_part
        kept_sum = kept_sum + keep
        exist_sum = exist_sum + present
    return (jnp.stack([total_row, total_col]), kept_sum, exist_sum)


def body(disp, velocity, bond_bits, panel_pos, contact_list):
    rows, cols = (disp.shape[1], disp.shape[2])
    along_count = lax.axis_size("along")
    across_count = lax.axis_size("across")
    total_rows = rows * along_count
    total_cols = cols * across_count
    row_base = lax.axis_index("along") * rows
    col_base = lax.axis_index("across") * cols
    state_u, state_v = (disp, velocity)
    damage = None
    for step in range(2):
        padded = with_halo(state_u, (("along", 1), ("across", 2)), 3)
        grid_row = row_base - 3 + jnp.arange(rows + 2 * 3, dtype=jnp.int32)
        grid_col = col_base - 3 + jnp.arange(cols + 2 * 3, dtype=jnp.int32)
        inside_row = (grid_row >= 0) & (grid_row < total_rows)
        inside_col = (grid_col >= 0) & (grid_col < total_cols)
        force, kept_sum, exist_sum = forces(
            padded,
            bond_bits,
            (inside_row[:, None] & inside_col[None, :]).astype(jnp.float32),
            rows,
            cols,
        )
        if step == 0:
            damage = 1.0 - kept_sum / exist_sum
        state_v = state_v + 10.0 * force
        state_u = state_u + 0.05 * state_v
    block_count = lax.axis_size("along")
    packed = jnp.concatenate(
        [panel_pos.reshape(1, -1), contact_list.astype(jnp.float32).reshape(1, -1)], axis=1
    )
    gathered = lax.all_gather(packed, "along", axis=0, tiled=True)
    all_pos = gathered[:, : 2 * PAN_DEV].reshape(block_count, PAN_DEV, 2)
    all_lists = gathered[:, 2 * PAN_DEV :].astype(jnp.int32)
    my_tile = lax.axis_index("along") * across_count + lax.axis_index("across")
    listed = jnp.any(all_lists == my_tile, axis=1).astype(jnp.int32)
    prefix = jnp.cumsum(listed)
    n_listed = prefix[-1]
    rows_x = (
        (row_base + jnp.arange(rows, dtype=jnp.int32)).astype(jnp.float32)[:, None] + state_u[0]
    ).reshape(-1)
    cols_x = (
        (col_base + jnp.arange(cols, dtype=jnp.int32)).astype(jnp.float32)[None, :] + state_u[1]
    ).reshape(-1)

    def one_block(k, acc):
        block = jnp.sum((prefix <= k).astype(jnp.int32))
        centre_blk = lax.dynamic_index_in_dim(all_pos, block, 0, keepdims=False)
        delta_row = centre_blk[:, 0:1] - rows_x[None, :]
        delta_col = centre_blk[:, 1:2] - cols_x[None, :]
        push = 0.5 * jnp.maximum(4.0 - delta_row * delta_row - delta_col * delta_col, 0.0)
        part = jnp.stack(
            [jnp.sum(push * delta_row, axis=1), jnp.sum(push * delta_col, axis=1)], axis=1
        )
        return lax.dynamic_update_index_in_dim(acc, part, block, 0)

    partials = lax.fori_loop(
        0, n_listed, one_block, jnp.zeros((block_count, PAN_DEV, 2), jnp.float32)
    )
    share = lax.psum_scatter(
        partials.reshape(block_count * PAN_DEV, 2),
        "along",
        scatter_dimension=0,
        tiled=True,
    )
    panel_force = lax.psum(share, "across")
    return (state_u, state_v, damage, panel_force)


def solution(mesh):
    return jax.shard_map(
        body,
        mesh=mesh,
        in_specs=(
            P(None, "along", "across"),
            P(None, "along", "across"),
            P(None, "along", "across"),
            P("along", None),
            P("along", None),
        ),
        out_specs=(
            P(None, "along", "across"),
            P(None, "along", "across"),
            P("along", "across"),
            P("along", None),
        ),
        check_vma=False,
    )
```

```python
import jax
import jax.numpy as jnp
from jax import lax
from jax.sharding import PartitionSpec as P

PAN_DEV = 64


offsets = [(rr, cc) for rr in range(-3, 4) for cc in range(-3, 4) if 0 < rr * rr + cc * cc <= 9]


def xor_pairs(count, bit):
    return [(i, i ^ (1 << bit)) for i in range(count)]


def with_halo(block, sides, width):
    for axis, dim in sides:
        count = lax.axis_size(axis)
        forward = [(i, i + 1) for i in range(count - 1)]
        backward = [(target, source) for source, target in forward]
        low = lax.ppermute(
            lax.slice_in_dim(block, block.shape[dim] - width, None, axis=dim), axis, forward
        )
        high = lax.ppermute(lax.slice_in_dim(block, 0, width, axis=dim), axis, backward)
        block = jnp.concatenate([low, block, high], axis=dim)
    return block


def forces(padded, bits, present_pad, rows, cols):
    centre = padded[:, 3 : 3 + rows, 3 : 3 + cols]
    total_row = jnp.zeros((rows, cols), jnp.float32)
    total_col = jnp.zeros((rows, cols), jnp.float32)
    kept_sum = jnp.zeros((rows, cols), jnp.float32)
    exist_sum = jnp.zeros((rows, cols), jnp.float32)
    for index, (row_off, col_off) in enumerate(offsets):
        other = padded[:, 3 + row_off : 3 + row_off + rows, 3 + col_off : 3 + col_off + cols]
        present = present_pad[3 + row_off : 3 + row_off + rows, 3 + col_off : 3 + col_off + cols]
        flag = jnp.bitwise_and(jnp.right_shift(bits[index // 14], index % 14), 1).astype(
            jnp.float32
        )
        keep = flag * present
        row_part = row_off + (other[0] - centre[0])
        col_part = col_off + (other[1] - centre[1])
        length = jnp.sqrt(row_part * row_part + col_part * col_part)
        rest = float((row_off * row_off + col_off * col_off) ** 0.5)
        coeff = keep * (length - rest) / (rest * length)
        total_row = total_row + coeff * row_part
        total_col = total_col + coeff * col_part
        kept_sum = kept_sum + keep
        exist_sum = exist_sum + present
    return (jnp.stack([total_row, total_col]), kept_sum, exist_sum)


def body(disp, velocity, bond_bits, panel_pos, contact_list):
    rows, cols = (disp.shape[1], disp.shape[2])
    along_count = lax.axis_size("along")
    across_count = lax.axis_size("across")
    total_rows = rows * along_count
    total_cols = cols * across_count
    row_base = lax.axis_index("along") * rows
    col_base = lax.axis_index("across") * cols
    state_u, state_v = (disp, velocity)
    damage = None
    for step in range(2):
        padded = with_halo(state_u, (("along", 1), ("across", 2)), 3)
        grid_row = row_base - 3 + jnp.arange(rows + 2 * 3, dtype=jnp.int32)
        grid_col = col_base - 3 + jnp.arange(cols + 2 * 3, dtype=jnp.int32)
        inside_row = (grid_row >= 0) & (grid_row < total_rows)
        inside_col = (grid_col >= 0) & (grid_col < total_cols)
        force, kept_sum, exist_sum = forces(
            padded,
            bond_bits,
            (inside_row[:, None] & inside_col[None, :]).astype(jnp.float32),
            rows,
            cols,
        )
        if step == 0:
            damage = 1.0 - kept_sum / exist_sum
        state_v = state_v + 10.0 * force
        state_u = state_u + 0.05 * state_v
    block_count = lax.axis_size("along")
    packed = jnp.concatenate(
        [panel_pos.reshape(1, -1), contact_list.astype(jnp.float32).reshape(1, -1)], axis=1
    )
    gathered = packed
    for k in range(block_count.bit_length() - 1):
        arrived = lax.ppermute(gathered, "along", xor_pairs(block_count, k))
        upper = ((lax.axis_index("along") >> k) & 1) == 1
        gathered = jnp.where(
            upper,
            jnp.concatenate([arrived, gathered], axis=0),
            jnp.concatenate([gathered, arrived], axis=0),
        )
    all_pos = gathered[:, : 2 * PAN_DEV].reshape(block_count, PAN_DEV, 2)
    all_lists = gathered[:, 2 * PAN_DEV :].astype(jnp.int32)
    my_tile = lax.axis_index("along") * across_count + lax.axis_index("across")
    listed = jnp.any(all_lists == my_tile, axis=1).astype(jnp.int32)
    prefix = jnp.cumsum(listed)
    n_listed = prefix[-1]
    rows_x = (
        (row_base + jnp.arange(rows, dtype=jnp.int32)).astype(jnp.float32)[:, None] + state_u[0]
    ).reshape(-1)
    cols_x = (
        (col_base + jnp.arange(cols, dtype=jnp.int32)).astype(jnp.float32)[None, :] + state_u[1]
    ).reshape(-1)

    def one_block(k, acc):
        block = jnp.sum((prefix <= k).astype(jnp.int32))
        centre_blk = lax.dynamic_index_in_dim(all_pos, block, 0, keepdims=False)
        delta_row = centre_blk[:, 0:1] - rows_x[None, :]
        delta_col = centre_blk[:, 1:2] - cols_x[None, :]
        push = 0.5 * jnp.maximum(4.0 - delta_row * delta_row - delta_col * delta_col, 0.0)
        part = jnp.stack(
            [jnp.sum(push * delta_row, axis=1), jnp.sum(push * delta_col, axis=1)], axis=1
        )
        return lax.dynamic_update_index_in_dim(acc, part, block, 0)

    partials = lax.fori_loop(
        0, n_listed, one_block, jnp.zeros((block_count, PAN_DEV, 2), jnp.float32)
    )
    arrived = lax.all_to_all(
        partials.reshape(block_count, 1, 2 * PAN_DEV), "along", 0, 0, tiled=True
    )
    share = jnp.sum(arrived, axis=0)
    for k in range(across_count.bit_length() - 1):
        share = share + lax.ppermute(share, "across", xor_pairs(across_count, k))
    panel_force = share.reshape(PAN_DEV, 2)
    return (state_u, state_v, damage, panel_force)


def solution(mesh):
    return jax.shard_map(
        body,
        mesh=mesh,
        in_specs=(
            P(None, "along", "across"),
            P(None, "along", "across"),
            P(None, "along", "across"),
            P("along", None),
            P("along", None),
        ),
        out_specs=(
            P(None, "along", "across"),
            P(None, "along", "across"),
            P("along", "across"),
            P("along", None),
        ),
        check_vma=False,
    )
```

```python
import jax
import jax.numpy as jnp
from jax import lax
from jax.experimental import pallas as pl
from jax.experimental.pallas import tpu as pltpu
from jax.sharding import PartitionSpec as P

PAN_DEV = 64


offsets = [(rr, cc) for rr in range(-3, 4) for cc in range(-3, 4) if 0 < rr * rr + cc * cc <= 9]


def xor_pairs(count, bit):
    return [(i, i ^ (1 << bit)) for i in range(count)]


def contact_kernel(meta_ref, win_ref, pos_ref, xr_ref, xc_ref, out_ref):
    out_ref[...] = jnp.zeros_like(out_ref)
    panels = out_ref.shape[2]

    def per_block(k, carry):
        block = meta_ref[1 + k]

        def per_panel(j, carry):
            slot = block * panels + j
            centre_row = pos_ref[2 * slot]
            centre_col = pos_ref[2 * slot + 1]
            first_row = win_ref[4 * slot]
            row_groups = win_ref[4 * slot + 1]
            first_col = win_ref[4 * slot + 2]
            col_groups = win_ref[4 * slot + 3]

            def per_row(r, accs):
                row = pl.multiple_of((first_row + r) * 8, 8)

                def per_col(c, accs):
                    col = pl.multiple_of((first_col + c) * 128, 128)
                    delta_row = centre_row - xr_ref[pl.ds(row, 8), pl.ds(col, 128)]
                    delta_col = centre_col - xc_ref[pl.ds(row, 8), pl.ds(col, 128)]
                    push = 0.5 * jnp.maximum(
                        4.0 - delta_row * delta_row - delta_col * delta_col, 0.0
                    )
                    return (accs[0] + push * delta_row, accs[1] + push * delta_col)

                return lax.fori_loop(0, col_groups, per_col, accs)

            zero = jnp.zeros((8, 128), jnp.float32)
            acc_row, acc_col = lax.fori_loop(0, row_groups, per_row, (zero, zero))
            out_ref[block, 0, pl.ds(j, 1), :] = jnp.sum(acc_row, axis=0, keepdims=True)
            out_ref[block, 1, pl.ds(j, 1), :] = jnp.sum(acc_col, axis=0, keepdims=True)
            return carry

        return lax.fori_loop(0, panels, per_panel, carry)

    lax.fori_loop(0, meta_ref[0], per_block, 0)


def contact_sums(meta, windows, positions, rows_x, cols_x):
    blocks = meta.shape[0] - 1
    smem = pl.BlockSpec(memory_space=pltpu.SMEM)
    vmem = pl.BlockSpec(memory_space=pltpu.VMEM)
    return pl.pallas_call(
        contact_kernel,
        out_shape=jax.ShapeDtypeStruct((blocks, 2, PAN_DEV, 128), jnp.float32),
        in_specs=[smem, smem, smem, vmem, vmem],
        out_specs=vmem,
    )(meta, windows, positions, rows_x, cols_x)


def with_halo(block, sides, width):
    for axis, dim in sides:
        count = lax.axis_size(axis)
        forward = [(i, i + 1) for i in range(count - 1)]
        backward = [(target, source) for source, target in forward]
        low = lax.ppermute(
            lax.slice_in_dim(block, block.shape[dim] - width, None, axis=dim), axis, forward
        )
        high = lax.ppermute(lax.slice_in_dim(block, 0, width, axis=dim), axis, backward)
        block = jnp.concatenate([low, block, high], axis=dim)
    return block


def forces(padded, bits, present_pad, rows, cols):
    centre = padded[:, 3 : 3 + rows, 3 : 3 + cols]
    total_row = jnp.zeros((rows, cols), jnp.float32)
    total_col = jnp.zeros((rows, cols), jnp.float32)
    kept_sum = jnp.zeros((rows, cols), jnp.float32)
    exist_sum = jnp.zeros((rows, cols), jnp.float32)
    for index, (row_off, col_off) in enumerate(offsets):
        other = padded[:, 3 + row_off : 3 + row_off + rows, 3 + col_off : 3 + col_off + cols]
        present = present_pad[3 + row_off : 3 + row_off + rows, 3 + col_off : 3 + col_off + cols]
        flag = jnp.bitwise_and(jnp.right_shift(bits[index // 14], index % 14), 1).astype(
            jnp.float32
        )
        keep = flag * present
        row_part = row_off + (other[0] - centre[0])
        col_part = col_off + (other[1] - centre[1])
        length = jnp.sqrt(row_part * row_part + col_part * col_part)
        rest = float((row_off * row_off + col_off * col_off) ** 0.5)
        coeff = keep * (length - rest) / (rest * length)
        total_row = total_row + coeff * row_part
        total_col = total_col + coeff * col_part
        kept_sum = kept_sum + keep
        exist_sum = exist_sum + present
    return (jnp.stack([total_row, total_col]), kept_sum, exist_sum)


def body(disp, velocity, bond_bits, panel_pos, contact_list):
    rows, cols = (disp.shape[1], disp.shape[2])
    along_count = lax.axis_size("along")
    across_count = lax.axis_size("across")
    total_rows = rows * along_count
    total_cols = cols * across_count
    row_base = lax.axis_index("along") * rows
    col_base = lax.axis_index("across") * cols
    state_u, state_v = (disp, velocity)
    damage = None
    for step in range(2):
        padded = with_halo(state_u, (("along", 1), ("across", 2)), 3)
        grid_row = row_base - 3 + jnp.arange(rows + 2 * 3, dtype=jnp.int32)
        grid_col = col_base - 3 + jnp.arange(cols + 2 * 3, dtype=jnp.int32)
        inside_row = (grid_row >= 0) & (grid_row < total_rows)
        inside_col = (grid_col >= 0) & (grid_col < total_cols)
        force, kept_sum, exist_sum = forces(
            padded,
            bond_bits,
            (inside_row[:, None] & inside_col[None, :]).astype(jnp.float32),
            rows,
            cols,
        )
        if step == 0:
            damage = 1.0 - kept_sum / exist_sum
        state_v = state_v + 10.0 * force
        state_u = state_u + 0.05 * state_v
    block_count = lax.axis_size("along")
    packed = jnp.concatenate(
        [panel_pos.reshape(1, -1), contact_list.astype(jnp.float32).reshape(1, -1)], axis=1
    )
    gathered = lax.all_to_all(
        jnp.broadcast_to(packed[None], (block_count,) + packed.shape), "along", 0, 0, tiled=True
    ).reshape(block_count, -1)
    all_pos = gathered[:, : 2 * PAN_DEV].reshape(block_count, PAN_DEV, 2)
    all_lists = gathered[:, 2 * PAN_DEV :].astype(jnp.int32)
    my_tile = lax.axis_index("along") * across_count + lax.axis_index("across")
    listed = jnp.any(all_lists == my_tile, axis=1).astype(jnp.int32)
    prefix = jnp.cumsum(listed)
    n_listed = prefix[-1]
    slots = jnp.arange(block_count, dtype=jnp.int32)
    listed_blocks = jnp.sum((prefix[None, :] <= slots[:, None]).astype(jnp.int32), axis=1)
    rows_x = (row_base + jnp.arange(rows, dtype=jnp.int32)).astype(jnp.float32)[:, None] + state_u[0]
    cols_x = (col_base + jnp.arange(cols, dtype=jnp.int32)).astype(jnp.float32)[None, :] + state_u[1]
    reach_row = 3.0 + jnp.max(jnp.abs(state_u[0]))
    reach_col = 3.0 + jnp.max(jnp.abs(state_u[1]))
    local_row = all_pos[:, :, 0] - row_base.astype(jnp.float32)
    local_col = all_pos[:, :, 1] - col_base.astype(jnp.float32)
    row_lo = jnp.clip(jnp.floor(local_row - reach_row), 0, rows).astype(jnp.int32)
    row_hi = jnp.clip(jnp.floor(local_row + reach_row) + 1, 0, rows).astype(jnp.int32)
    col_lo = jnp.clip(jnp.floor(local_col - reach_col), 0, cols).astype(jnp.int32)
    col_hi = jnp.clip(jnp.floor(local_col + reach_col) + 1, 0, cols).astype(jnp.int32)
    first_row = row_lo // 8
    row_groups = jnp.maximum((row_hi + 7) // 8 - first_row, 0)
    first_col = col_lo // 128
    col_groups = jnp.maximum((col_hi + 127) // 128 - first_col, 0)
    windows = jnp.stack([first_row, row_groups, first_col, col_groups], axis=-1).reshape(-1)
    meta = jnp.concatenate([n_listed[None], listed_blocks])
    sums = contact_sums(meta, windows, all_pos.reshape(-1), rows_x, cols_x)
    partials = jnp.transpose(jnp.sum(sums, axis=-1), (0, 2, 1))
    arrived = lax.all_to_all(
        partials.reshape(block_count, 1, 2 * PAN_DEV), "along", 0, 0, tiled=True
    )
    share = jnp.sum(arrived, axis=0)
    for k in range(across_count.bit_length() - 1):
        share = share + lax.ppermute(share, "across", xor_pairs(across_count, k))
    panel_force = share.reshape(PAN_DEV, 2)
    return (state_u, state_v, damage, panel_force)


def solution(mesh):
    return jax.shard_map(
        body,
        mesh=mesh,
        in_specs=(
            P(None, "along", "across"),
            P(None, "along", "across"),
            P(None, "along", "across"),
            P("along", None),
            P("along", None),
        ),
        out_specs=(
            P(None, "along", "across"),
            P(None, "along", "across"),
            P("along", "across"),
            P("along", None),
        ),
        check_vma=False,
    )
```

```python
import jax
import jax.numpy as jnp
from jax import lax
from jax.experimental import pallas as pl
from jax.experimental.pallas import tpu as pltpu
from jax.sharding import PartitionSpec as P

PAN_DEV = 64


offsets = [(rr, cc) for rr in range(-3, 4) for cc in range(-3, 4) if 0 < rr * rr + cc * cc <= 9]


def contact_kernel(meta_ref, win_ref, pos_ref, xr_ref, xc_ref, out_ref):
    out_ref[...] = jnp.zeros_like(out_ref)
    panels = out_ref.shape[2]

    def per_block(k, carry):
        block = meta_ref[1 + k]

        def per_panel(j, carry):
            slot = block * panels + j
            centre_row = pos_ref[2 * slot]
            centre_col = pos_ref[2 * slot + 1]
            first_row = win_ref[4 * slot]
            row_groups = win_ref[4 * slot + 1]
            first_col = win_ref[4 * slot + 2]
            col_groups = win_ref[4 * slot + 3]

            def per_row(r, accs):
                row = pl.multiple_of((first_row + r) * 8, 8)

                def per_col(c, accs):
                    col = pl.multiple_of((first_col + c) * 128, 128)
                    delta_row = centre_row - xr_ref[pl.ds(row, 8), pl.ds(col, 128)]
                    delta_col = centre_col - xc_ref[pl.ds(row, 8), pl.ds(col, 128)]
                    push = 0.5 * jnp.maximum(
                        4.0 - delta_row * delta_row - delta_col * delta_col, 0.0
                    )
                    return (accs[0] + push * delta_row, accs[1] + push * delta_col)

                return lax.fori_loop(0, col_groups, per_col, accs)

            zero = jnp.zeros((8, 128), jnp.float32)
            acc_row, acc_col = lax.fori_loop(0, row_groups, per_row, (zero, zero))
            out_ref[block, 0, pl.ds(j, 1), :] = jnp.sum(acc_row, axis=0, keepdims=True)
            out_ref[block, 1, pl.ds(j, 1), :] = jnp.sum(acc_col, axis=0, keepdims=True)
            return carry

        return lax.fori_loop(0, panels, per_panel, carry)

    lax.fori_loop(0, meta_ref[0], per_block, 0)


def contact_sums(meta, windows, positions, rows_x, cols_x):
    blocks = meta.shape[0] - 1
    smem = pl.BlockSpec(memory_space=pltpu.SMEM)
    vmem = pl.BlockSpec(memory_space=pltpu.VMEM)
    return pl.pallas_call(
        contact_kernel,
        out_shape=jax.ShapeDtypeStruct((blocks, 2, PAN_DEV, 128), jnp.float32),
        in_specs=[smem, smem, smem, vmem, vmem],
        out_specs=vmem,
    )(meta, windows, positions, rows_x, cols_x)


def with_halo(block, sides, width):
    for axis, dim in sides:
        count = lax.axis_size(axis)
        forward = [(i, i + 1) for i in range(count - 1)]
        backward = [(target, source) for source, target in forward]
        low = lax.ppermute(
            lax.slice_in_dim(block, block.shape[dim] - width, None, axis=dim), axis, forward
        )
        high = lax.ppermute(lax.slice_in_dim(block, 0, width, axis=dim), axis, backward)
        block = jnp.concatenate([low, block, high], axis=dim)
    return block


def forces(padded, bits, present_pad, rows, cols):
    centre = padded[:, 3 : 3 + rows, 3 : 3 + cols]
    total_row = jnp.zeros((rows, cols), jnp.float32)
    total_col = jnp.zeros((rows, cols), jnp.float32)
    kept_sum = jnp.zeros((rows, cols), jnp.float32)
    exist_sum = jnp.zeros((rows, cols), jnp.float32)
    for index, (row_off, col_off) in enumerate(offsets):
        other = padded[:, 3 + row_off : 3 + row_off + rows, 3 + col_off : 3 + col_off + cols]
        present = present_pad[3 + row_off : 3 + row_off + rows, 3 + col_off : 3 + col_off + cols]
        flag = jnp.bitwise_and(jnp.right_shift(bits[index // 14], index % 14), 1).astype(
            jnp.float32
        )
        keep = flag * present
        row_part = row_off + (other[0] - centre[0])
        col_part = col_off + (other[1] - centre[1])
        length = jnp.sqrt(row_part * row_part + col_part * col_part)
        rest = float((row_off * row_off + col_off * col_off) ** 0.5)
        coeff = keep * (length - rest) / (rest * length)
        total_row = total_row + coeff * row_part
        total_col = total_col + coeff * col_part
        kept_sum = kept_sum + keep
        exist_sum = exist_sum + present
    return (jnp.stack([total_row, total_col]), kept_sum, exist_sum)


def body(disp, velocity, bond_bits, panel_pos, contact_list):
    rows, cols = (disp.shape[1], disp.shape[2])
    along_count = lax.axis_size("along")
    across_count = lax.axis_size("across")
    total_rows = rows * along_count
    total_cols = cols * across_count
    row_base = lax.axis_index("along") * rows
    col_base = lax.axis_index("across") * cols
    stacked = jnp.concatenate([disp, velocity, bond_bits.astype(jnp.float32)], axis=0)
    ext = with_halo(stacked, (("along", 1), ("across", 2)), 6)
    grid_row = row_base - 6 + jnp.arange(rows + 12, dtype=jnp.int32)
    grid_col = col_base - 6 + jnp.arange(cols + 12, dtype=jnp.int32)
    inside_row = (grid_row >= 0) & (grid_row < total_rows)
    inside_col = (grid_col >= 0) & (grid_col < total_cols)
    present_wide = (inside_row[:, None] & inside_col[None, :]).astype(jnp.float32)
    present_ring = present_wide[3:-3, 3:-3]
    force, kept_sum, exist_sum = forces(
        ext[0:2], ext[4:6, 3:-3, 3:-3].astype(jnp.int32), present_wide, rows + 6, cols + 6
    )
    damage = 1.0 - kept_sum[3:-3, 3:-3] / exist_sum[3:-3, 3:-3]
    ring_v = ext[2:4, 3:-3, 3:-3] + 10.0 * force
    ring_u = ext[0:2, 3:-3, 3:-3] + 0.05 * ring_v
    ring_u = jnp.where(present_ring[None] > 0.0, ring_u, 0.0)
    force, _, _ = forces(ring_u, bond_bits, present_ring, rows, cols)
    state_v = ring_v[:, 3:-3, 3:-3] + 10.0 * force
    state_u = ring_u[:, 3:-3, 3:-3] + 0.05 * state_v
    block_count = lax.axis_size("along")
    packed = jnp.concatenate(
        [panel_pos.reshape(1, -1), contact_list.astype(jnp.float32).reshape(1, -1)], axis=1
    )
    gathered = lax.all_to_all(
        jnp.broadcast_to(packed[None], (block_count,) + packed.shape), "along", 0, 0, tiled=True
    ).reshape(block_count, -1)
    all_pos = gathered[:, : 2 * PAN_DEV].reshape(block_count, PAN_DEV, 2)
    all_lists = gathered[:, 2 * PAN_DEV :].astype(jnp.int32)
    my_tile = lax.axis_index("along") * across_count + lax.axis_index("across")
    listed = jnp.any(all_lists == my_tile, axis=1).astype(jnp.int32)
    prefix = jnp.cumsum(listed)
    n_listed = prefix[-1]
    slots = jnp.arange(block_count, dtype=jnp.int32)
    listed_blocks = jnp.sum((prefix[None, :] <= slots[:, None]).astype(jnp.int32), axis=1)
    rows_x = (row_base + jnp.arange(rows, dtype=jnp.int32)).astype(jnp.float32)[:, None] + state_u[0]
    cols_x = (col_base + jnp.arange(cols, dtype=jnp.int32)).astype(jnp.float32)[None, :] + state_u[1]
    reach_row = 3.0 + jnp.max(jnp.abs(state_u[0]))
    reach_col = 3.0 + jnp.max(jnp.abs(state_u[1]))
    local_row = all_pos[:, :, 0] - row_base.astype(jnp.float32)
    local_col = all_pos[:, :, 1] - col_base.astype(jnp.float32)
    row_lo = jnp.clip(jnp.floor(local_row - reach_row), 0, rows).astype(jnp.int32)
    row_hi = jnp.clip(jnp.floor(local_row + reach_row) + 1, 0, rows).astype(jnp.int32)
    col_lo = jnp.clip(jnp.floor(local_col - reach_col), 0, cols).astype(jnp.int32)
    col_hi = jnp.clip(jnp.floor(local_col + reach_col) + 1, 0, cols).astype(jnp.int32)
    first_row = row_lo // 8
    row_groups = jnp.maximum((row_hi + 7) // 8 - first_row, 0)
    first_col = col_lo // 128
    col_groups = jnp.maximum((col_hi + 127) // 128 - first_col, 0)
    windows = jnp.stack([first_row, row_groups, first_col, col_groups], axis=-1).reshape(-1)
    meta = jnp.concatenate([n_listed[None], listed_blocks])
    sums = contact_sums(meta, windows, all_pos.reshape(-1), rows_x, cols_x)
    partials = jnp.transpose(jnp.sum(sums, axis=-1), (0, 2, 1))
    spread = jnp.broadcast_to(
        partials.reshape(block_count, 1, 1, 2 * PAN_DEV),
        (block_count, across_count, 1, 2 * PAN_DEV),
    ).reshape(block_count * across_count, 1, 2 * PAN_DEV)
    arrived = lax.all_to_all(spread, ("along", "across"), 0, 0, tiled=True)
    panel_force = jnp.sum(arrived, axis=0).reshape(PAN_DEV, 2)
    return (state_u, state_v, damage, panel_force)


def solution(mesh):
    return jax.shard_map(
        body,
        mesh=mesh,
        in_specs=(
            P(None, "along", "across"),
            P(None, "along", "across"),
            P(None, "along", "across"),
            P("along", None),
            P("along", None),
        ),
        out_specs=(
            P(None, "along", "across"),
            P(None, "along", "across"),
            P("along", "across"),
            P("along", None),
        ),
        check_vma=False,
    )
```

```python
import jax
import jax.numpy as jnp
from jax import lax
from jax.experimental import pallas as pl
from jax.experimental.pallas import tpu as pltpu
from jax.sharding import PartitionSpec as P

PAN_DEV = 64


offsets = [(rr, cc) for rr in range(-3, 4) for cc in range(-3, 4) if 0 < rr * rr + cc * cc <= 9]


def contact_kernel(meta_ref, win_ref, pos_ref, xr_ref, xc_ref, out_ref):
    out_ref[...] = jnp.zeros_like(out_ref)
    panels = out_ref.shape[2]

    def per_block(k, carry):
        block = meta_ref[1 + k]

        def per_panel(j, carry):
            slot = block * panels + j
            centre_row = pos_ref[2 * slot]
            centre_col = pos_ref[2 * slot + 1]
            first_row = win_ref[4 * slot]
            row_groups = win_ref[4 * slot + 1]
            first_col = win_ref[4 * slot + 2]
            col_groups = win_ref[4 * slot + 3]

            def per_row(r, accs):
                row = pl.multiple_of((first_row + r) * 8, 8)

                def per_col(c, accs):
                    col = pl.multiple_of((first_col + c) * 128, 128)
                    delta_row = centre_row - xr_ref[pl.ds(row, 8), pl.ds(col, 128)]
                    delta_col = centre_col - xc_ref[pl.ds(row, 8), pl.ds(col, 128)]
                    push = 0.5 * jnp.maximum(
                        4.0 - delta_row * delta_row - delta_col * delta_col, 0.0
                    )
                    return (accs[0] + push * delta_row, accs[1] + push * delta_col)

                return lax.fori_loop(0, col_groups, per_col, accs)

            zero = jnp.zeros((8, 128), jnp.float32)
            acc_row, acc_col = lax.fori_loop(0, row_groups, per_row, (zero, zero))
            out_ref[block, 0, pl.ds(j, 1), :] = jnp.sum(acc_row, axis=0, keepdims=True)
            out_ref[block, 1, pl.ds(j, 1), :] = jnp.sum(acc_col, axis=0, keepdims=True)
            return carry

        return lax.fori_loop(0, panels, per_panel, carry)

    lax.fori_loop(0, meta_ref[0], per_block, 0)


def contact_sums(meta, windows, positions, rows_x, cols_x):
    blocks = meta.shape[0] - 1
    smem = pl.BlockSpec(memory_space=pltpu.SMEM)
    vmem = pl.BlockSpec(memory_space=pltpu.VMEM)
    return pl.pallas_call(
        contact_kernel,
        out_shape=jax.ShapeDtypeStruct((blocks, 2, PAN_DEV, 128), jnp.float32),
        in_specs=[smem, smem, smem, vmem, vmem],
        out_specs=vmem,
    )(meta, windows, positions, rows_x, cols_x)


def with_halo(block, sides, width):
    for axis, dim in sides:
        count = lax.axis_size(axis)
        forward = [(i, i + 1) for i in range(count - 1)]
        backward = [(target, source) for source, target in forward]
        narrow = dim == block.ndim - 1
        low = lax.slice_in_dim(block, block.shape[dim] - width, None, axis=dim)
        high = lax.slice_in_dim(block, 0, width, axis=dim)
        strip = low.shape
        if narrow:
            low, high = low.reshape(-1), high.reshape(-1)
        low = lax.ppermute(low, axis, forward).reshape(strip)
        high = lax.ppermute(high, axis, backward).reshape(strip)
        block = jnp.concatenate([low, block, high], axis=dim)
    return block


def forces(padded, bits, present_pad, rows, cols):
    centre = padded[:, 3 : 3 + rows, 3 : 3 + cols]
    total_row = jnp.zeros((rows, cols), jnp.float32)
    total_col = jnp.zeros((rows, cols), jnp.float32)
    kept_sum = jnp.zeros((rows, cols), jnp.float32)
    exist_sum = jnp.zeros((rows, cols), jnp.float32)
    for index, (row_off, col_off) in enumerate(offsets):
        other = padded[:, 3 + row_off : 3 + row_off + rows, 3 + col_off : 3 + col_off + cols]
        present = present_pad[3 + row_off : 3 + row_off + rows, 3 + col_off : 3 + col_off + cols]
        flag = jnp.bitwise_and(jnp.right_shift(bits[index // 14], index % 14), 1).astype(
            jnp.float32
        )
        keep = flag * present
        row_part = row_off + (other[0] - centre[0])
        col_part = col_off + (other[1] - centre[1])
        length = jnp.sqrt(row_part * row_part + col_part * col_part)
        rest = float((row_off * row_off + col_off * col_off) ** 0.5)
        coeff = keep * (length - rest) / (rest * length)
        total_row = total_row + coeff * row_part
        total_col = total_col + coeff * col_part
        kept_sum = kept_sum + keep
        exist_sum = exist_sum + present
    return (jnp.stack([total_row, total_col]), kept_sum, exist_sum)


def body(disp, velocity, bond_bits, panel_pos, contact_list):
    rows, cols = (disp.shape[1], disp.shape[2])
    along_count = lax.axis_size("along")
    across_count = lax.axis_size("across")
    total_rows = rows * along_count
    total_cols = cols * across_count
    row_base = lax.axis_index("along") * rows
    col_base = lax.axis_index("across") * cols
    stacked = jnp.concatenate([disp, velocity, bond_bits.astype(jnp.float32)], axis=0)
    ext = with_halo(stacked, (("along", 1), ("across", 2)), 6)
    grid_row = row_base - 6 + jnp.arange(rows + 12, dtype=jnp.int32)
    grid_col = col_base - 6 + jnp.arange(cols + 12, dtype=jnp.int32)
    inside_row = (grid_row >= 0) & (grid_row < total_rows)
    inside_col = (grid_col >= 0) & (grid_col < total_cols)
    present_wide = (inside_row[:, None] & inside_col[None, :]).astype(jnp.float32)
    present_ring = present_wide[3:-3, 3:-3]
    force, kept_sum, exist_sum = forces(
        ext[0:2], ext[4:6, 3:-3, 3:-3].astype(jnp.int32), present_wide, rows + 6, cols + 6
    )
    damage = 1.0 - kept_sum[3:-3, 3:-3] / exist_sum[3:-3, 3:-3]
    ring_v = ext[2:4, 3:-3, 3:-3] + 10.0 * force
    ring_u = ext[0:2, 3:-3, 3:-3] + 0.05 * ring_v
    ring_u = jnp.where(present_ring[None] > 0.0, ring_u, 0.0)
    force, _, _ = forces(ring_u, bond_bits, present_ring, rows, cols)
    state_v = ring_v[:, 3:-3, 3:-3] + 10.0 * force
    state_u = ring_u[:, 3:-3, 3:-3] + 0.05 * state_v
    block_count = lax.axis_size("along")
    packed = jnp.concatenate(
        [panel_pos.reshape(1, -1), contact_list.astype(jnp.float32).reshape(1, -1)], axis=1
    )
    gathered = lax.all_to_all(
        jnp.broadcast_to(packed[None], (block_count,) + packed.shape), "along", 0, 0, tiled=True
    ).reshape(block_count, -1)
    all_pos = gathered[:, : 2 * PAN_DEV].reshape(block_count, PAN_DEV, 2)
    all_lists = gathered[:, 2 * PAN_DEV :].astype(jnp.int32)
    my_tile = lax.axis_index("along") * across_count + lax.axis_index("across")
    listed = jnp.any(all_lists == my_tile, axis=1).astype(jnp.int32)
    prefix = jnp.cumsum(listed)
    n_listed = prefix[-1]
    slots = jnp.arange(block_count, dtype=jnp.int32)
    listed_blocks = jnp.sum((prefix[None, :] <= slots[:, None]).astype(jnp.int32), axis=1)
    rows_x = (row_base + jnp.arange(rows, dtype=jnp.int32)).astype(jnp.float32)[:, None] + state_u[0]
    cols_x = (col_base + jnp.arange(cols, dtype=jnp.int32)).astype(jnp.float32)[None, :] + state_u[1]
    reach_row = 3.0 + jnp.max(jnp.abs(state_u[0]))
    reach_col = 3.0 + jnp.max(jnp.abs(state_u[1]))
    local_row = all_pos[:, :, 0] - row_base.astype(jnp.float32)
    local_col = all_pos[:, :, 1] - col_base.astype(jnp.float32)
    row_lo = jnp.clip(jnp.floor(local_row - reach_row), 0, rows).astype(jnp.int32)
    row_hi = jnp.clip(jnp.floor(local_row + reach_row) + 1, 0, rows).astype(jnp.int32)
    col_lo = jnp.clip(jnp.floor(local_col - reach_col), 0, cols).astype(jnp.int32)
    col_hi = jnp.clip(jnp.floor(local_col + reach_col) + 1, 0, cols).astype(jnp.int32)
    first_row = row_lo // 8
    row_groups = jnp.maximum((row_hi + 7) // 8 - first_row, 0)
    first_col = col_lo // 128
    col_groups = jnp.maximum((col_hi + 127) // 128 - first_col, 0)
    windows = jnp.stack([first_row, row_groups, first_col, col_groups], axis=-1).reshape(-1)
    meta = jnp.concatenate([n_listed[None], listed_blocks])
    sums = contact_sums(meta, windows, all_pos.reshape(-1), rows_x, cols_x)
    partials = jnp.transpose(jnp.sum(sums, axis=-1), (0, 2, 1))
    spread = jnp.broadcast_to(
        partials.reshape(block_count, 1, 1, 2 * PAN_DEV),
        (block_count, across_count, 1, 2 * PAN_DEV),
    ).reshape(block_count * across_count, 1, 2 * PAN_DEV)
    arrived = lax.all_to_all(spread, ("along", "across"), 0, 0, tiled=True)
    panel_force = jnp.sum(arrived, axis=0).reshape(PAN_DEV, 2)
    return (state_u, state_v, damage, panel_force)


def solution(mesh):
    return jax.shard_map(
        body,
        mesh=mesh,
        in_specs=(
            P(None, "along", "across"),
            P(None, "along", "across"),
            P(None, "along", "across"),
            P("along", None),
            P("along", None),
        ),
        out_specs=(
            P(None, "along", "across"),
            P(None, "along", "across"),
            P("along", "across"),
            P("along", None),
        ),
        check_vma=False,
    )
```

```python
import jax
import jax.numpy as jnp
from jax import lax
from jax.experimental import pallas as pl
from jax.experimental.pallas import tpu as pltpu
from jax.sharding import PartitionSpec as P

PAN_DEV = 64


offsets = [(rr, cc) for rr in range(-3, 4) for cc in range(-3, 4) if 0 < rr * rr + cc * cc <= 9]


def contact_kernel(meta_ref, win_ref, pos_ref, xr_ref, xc_ref, out_ref):
    out_ref[...] = jnp.zeros_like(out_ref)
    blocks, _, panels, _ = out_ref.shape
    row_tiles = xr_ref.shape[0] // 8
    col_tiles = xr_ref.shape[1] // 128

    def tile_sums(centre_row, centre_col, row_group, col_group, accs):
        row = pl.multiple_of(row_group * 8, 8)
        col = pl.multiple_of(col_group * 128, 128)
        delta_row = centre_row - xr_ref[pl.ds(row, 8), pl.ds(col, 128)]
        delta_col = centre_col - xc_ref[pl.ds(row, 8), pl.ds(col, 128)]
        push = 0.5 * jnp.maximum(4.0 - delta_row * delta_row - delta_col * delta_col, 0.0)
        return (accs[0] + push * delta_row, accs[1] + push * delta_col)

    def store(block, j, accs):
        out_ref[block, 0, pl.ds(j, 1), :] = jnp.sum(accs[0], axis=0, keepdims=True)
        out_ref[block, 1, pl.ds(j, 1), :] = jnp.sum(accs[1], axis=0, keepdims=True)

    zero = jnp.zeros((8, 128), jnp.float32)

    def per_block_narrow(k, carry):
        block = meta_ref[1 + k]

        def per_panel(j, carry):
            slot = block * panels + j
            centre_row = pos_ref[2 * slot]
            centre_col = pos_ref[2 * slot + 1]
            first_row = jnp.minimum(win_ref[4 * slot], row_tiles - 2)
            first_col = jnp.minimum(win_ref[4 * slot + 2], col_tiles - 2)
            accs = (zero, zero)
            for r in range(2):
                for c in range(2):
                    accs = tile_sums(centre_row, centre_col, first_row + r, first_col + c, accs)
            store(block, j, accs)
            return carry

        return lax.fori_loop(0, panels, per_panel, carry, unroll=4)

    def per_block_wide(k, carry):
        block = meta_ref[1 + k]

        def per_panel(j, carry):
            slot = block * panels + j
            centre_row = pos_ref[2 * slot]
            centre_col = pos_ref[2 * slot + 1]
            first_row = win_ref[4 * slot]
            row_groups = win_ref[4 * slot + 1]
            first_col = win_ref[4 * slot + 2]
            col_groups = win_ref[4 * slot + 3]

            def per_row(r, accs):
                def per_col(c, accs):
                    return tile_sums(centre_row, centre_col, first_row + r, first_col + c, accs)

                return lax.fori_loop(0, col_groups, per_col, accs)

            store(block, j, lax.fori_loop(0, row_groups, per_row, (zero, zero)))
            return carry

        return lax.fori_loop(0, panels, per_panel, carry)

    narrow = meta_ref[1 + blocks]

    @pl.when(narrow == 1)
    def _():
        lax.fori_loop(0, meta_ref[0], per_block_narrow, 0)

    @pl.when(narrow == 0)
    def _():
        lax.fori_loop(0, meta_ref[0], per_block_wide, 0)


def contact_sums(meta, windows, positions, rows_x, cols_x):
    blocks = meta.shape[0] - 2
    smem = pl.BlockSpec(memory_space=pltpu.SMEM)
    vmem = pl.BlockSpec(memory_space=pltpu.VMEM)
    return pl.pallas_call(
        contact_kernel,
        out_shape=jax.ShapeDtypeStruct((blocks, 2, PAN_DEV, 128), jnp.float32),
        in_specs=[smem, smem, smem, vmem, vmem],
        out_specs=vmem,
    )(meta, windows, positions, rows_x, cols_x)


def with_halo(block, sides, width):
    for axis, dim in sides:
        count = lax.axis_size(axis)
        forward = [(i, i + 1) for i in range(count - 1)]
        backward = [(target, source) for source, target in forward]
        narrow = dim == block.ndim - 1
        low = lax.slice_in_dim(block, block.shape[dim] - width, None, axis=dim)
        high = lax.slice_in_dim(block, 0, width, axis=dim)
        strip = low.shape
        if narrow:
            low, high = low.reshape(-1), high.reshape(-1)
        low = lax.ppermute(low, axis, forward).reshape(strip)
        high = lax.ppermute(high, axis, backward).reshape(strip)
        block = jnp.concatenate([low, block, high], axis=dim)
    return block


def forces(padded, bits, present_pad, rows, cols):
    centre = padded[:, 3 : 3 + rows, 3 : 3 + cols]
    total_row = jnp.zeros((rows, cols), jnp.float32)
    total_col = jnp.zeros((rows, cols), jnp.float32)
    kept_sum = jnp.zeros((rows, cols), jnp.float32)
    exist_sum = jnp.zeros((rows, cols), jnp.float32)
    for index, (row_off, col_off) in enumerate(offsets):
        other = padded[:, 3 + row_off : 3 + row_off + rows, 3 + col_off : 3 + col_off + cols]
        present = present_pad[3 + row_off : 3 + row_off + rows, 3 + col_off : 3 + col_off + cols]
        flag = jnp.bitwise_and(jnp.right_shift(bits[index // 14], index % 14), 1).astype(
            jnp.float32
        )
        keep = flag * present
        row_part = row_off + (other[0] - centre[0])
        col_part = col_off + (other[1] - centre[1])
        length = jnp.sqrt(row_part * row_part + col_part * col_part)
        rest = float((row_off * row_off + col_off * col_off) ** 0.5)
        coeff = keep * (length - rest) / (rest * length)
        total_row = total_row + coeff * row_part
        total_col = total_col + coeff * col_part
        kept_sum = kept_sum + keep
        exist_sum = exist_sum + present
    return (jnp.stack([total_row, total_col]), kept_sum, exist_sum)


def body(disp, velocity, bond_bits, panel_pos, contact_list):
    rows, cols = (disp.shape[1], disp.shape[2])
    along_count = lax.axis_size("along")
    across_count = lax.axis_size("across")
    total_rows = rows * along_count
    total_cols = cols * across_count
    row_base = lax.axis_index("along") * rows
    col_base = lax.axis_index("across") * cols
    stacked = jnp.concatenate([disp, velocity, bond_bits.astype(jnp.float32)], axis=0)
    ext = with_halo(stacked, (("along", 1), ("across", 2)), 6)
    grid_row = row_base - 6 + jnp.arange(rows + 12, dtype=jnp.int32)
    grid_col = col_base - 6 + jnp.arange(cols + 12, dtype=jnp.int32)
    inside_row = (grid_row >= 0) & (grid_row < total_rows)
    inside_col = (grid_col >= 0) & (grid_col < total_cols)
    present_wide = (inside_row[:, None] & inside_col[None, :]).astype(jnp.float32)
    present_ring = present_wide[3:-3, 3:-3]
    force, kept_sum, exist_sum = forces(
        ext[0:2], ext[4:6, 3:-3, 3:-3].astype(jnp.int32), present_wide, rows + 6, cols + 6
    )
    damage = 1.0 - kept_sum[3:-3, 3:-3] / exist_sum[3:-3, 3:-3]
    ring_v = ext[2:4, 3:-3, 3:-3] + 10.0 * force
    ring_u = ext[0:2, 3:-3, 3:-3] + 0.05 * ring_v
    ring_u = jnp.where(present_ring[None] > 0.0, ring_u, 0.0)
    force, _, _ = forces(ring_u, bond_bits, present_ring, rows, cols)
    state_v = ring_v[:, 3:-3, 3:-3] + 10.0 * force
    state_u = ring_u[:, 3:-3, 3:-3] + 0.05 * state_v
    block_count = lax.axis_size("along")
    packed = jnp.concatenate(
        [panel_pos.reshape(1, -1), contact_list.astype(jnp.float32).reshape(1, -1)], axis=1
    )
    gathered = lax.all_to_all(
        jnp.broadcast_to(packed[None], (block_count,) + packed.shape), "along", 0, 0, tiled=True
    ).reshape(block_count, -1)
    all_pos = gathered[:, : 2 * PAN_DEV].reshape(block_count, PAN_DEV, 2)
    all_lists = gathered[:, 2 * PAN_DEV :].astype(jnp.int32)
    my_tile = lax.axis_index("along") * across_count + lax.axis_index("across")
    listed = jnp.any(all_lists == my_tile, axis=1).astype(jnp.int32)
    prefix = jnp.cumsum(listed)
    n_listed = prefix[-1]
    slots = jnp.arange(block_count, dtype=jnp.int32)
    listed_blocks = jnp.sum((prefix[None, :] <= slots[:, None]).astype(jnp.int32), axis=1)
    rows_x = (row_base + jnp.arange(rows, dtype=jnp.int32)).astype(jnp.float32)[:, None] + state_u[0]
    cols_x = (col_base + jnp.arange(cols, dtype=jnp.int32)).astype(jnp.float32)[None, :] + state_u[1]
    reach_row = 2.5 + jnp.max(jnp.abs(state_u[0]))
    reach_col = 2.5 + jnp.max(jnp.abs(state_u[1]))
    local_row = all_pos[:, :, 0] - row_base.astype(jnp.float32)
    local_col = all_pos[:, :, 1] - col_base.astype(jnp.float32)
    row_lo = jnp.clip(jnp.floor(local_row - reach_row), 0, rows).astype(jnp.int32)
    row_hi = jnp.clip(jnp.floor(local_row + reach_row) + 1, 0, rows).astype(jnp.int32)
    col_lo = jnp.clip(jnp.floor(local_col - reach_col), 0, cols).astype(jnp.int32)
    col_hi = jnp.clip(jnp.floor(local_col + reach_col) + 1, 0, cols).astype(jnp.int32)
    first_row = row_lo // 8
    row_groups = jnp.maximum((row_hi + 7) // 8 - first_row, 0)
    first_col = col_lo // 128
    col_groups = jnp.maximum((col_hi + 127) // 128 - first_col, 0)
    windows = jnp.stack([first_row, row_groups, first_col, col_groups], axis=-1).reshape(-1)
    narrow = (jnp.max(row_groups) <= 2) & (jnp.max(col_groups) <= 2)
    meta = jnp.concatenate([n_listed[None], listed_blocks, narrow.astype(jnp.int32)[None]])
    sums = contact_sums(meta, windows, all_pos.reshape(-1), rows_x, cols_x)
    partials = jnp.transpose(jnp.sum(sums, axis=-1), (0, 2, 1))
    spread = jnp.broadcast_to(
        partials.reshape(block_count, 1, 1, 2 * PAN_DEV),
        (block_count, across_count, 1, 2 * PAN_DEV),
    ).reshape(block_count * across_count, 1, 2 * PAN_DEV)
    arrived = lax.all_to_all(spread, ("along", "across"), 0, 0, tiled=True)
    panel_force = jnp.sum(arrived, axis=0).reshape(PAN_DEV, 2)
    return (state_u, state_v, damage, panel_force)


def solution(mesh):
    return jax.shard_map(
        body,
        mesh=mesh,
        in_specs=(
            P(None, "along", "across"),
            P(None, "along", "across"),
            P(None, "along", "across"),
            P("along", None),
            P("along", None),
        ),
        out_specs=(
            P(None, "along", "across"),
            P(None, "along", "across"),
            P("along", "across"),
            P("along", None),
        ),
        check_vma=False,
    )
```

```python
import jax
import jax.numpy as jnp
from jax import lax
from jax.experimental import pallas as pl
from jax.experimental.pallas import tpu as pltpu
from jax.sharding import PartitionSpec as P

PAN_DEV = 64


offsets = [(rr, cc) for rr in range(-3, 4) for cc in range(-3, 4) if 0 < rr * rr + cc * cc <= 9]


def contact_kernel(meta_ref, geo_ref, pos_ref, xr_ref, xc_ref, out_ref):
    out_ref[...] = jnp.zeros_like(out_ref)
    blocks, _, panels, _ = out_ref.shape
    rows, cols = xr_ref.shape
    row_tiles = rows // 8
    col_tiles = cols // 128
    reach_row, reach_col = geo_ref[0], geo_ref[1]
    row_base, col_base = geo_ref[2], geo_ref[3]

    def window(centre, base, reach, size, group):
        local = centre - base
        low = jnp.clip((local - reach).astype(jnp.int32), 0, size)
        high = jnp.clip((local + reach).astype(jnp.int32) + 1, 0, size)
        first = low // group
        return first, jnp.maximum((high + group - 1) // group - first, 0)

    def tile_sums(centre_row, centre_col, row_group, col_group, accs):
        row = pl.multiple_of(row_group * 8, 8)
        col = pl.multiple_of(col_group * 128, 128)
        delta_row = centre_row - xr_ref[pl.ds(row, 8), pl.ds(col, 128)]
        delta_col = centre_col - xc_ref[pl.ds(row, 8), pl.ds(col, 128)]
        push = 0.5 * jnp.maximum(4.0 - delta_row * delta_row - delta_col * delta_col, 0.0)
        return (accs[0] + push * delta_row, accs[1] + push * delta_col)

    def store(block, j, accs):
        out_ref[block, 0, pl.ds(j, 1), :] = jnp.sum(accs[0], axis=0, keepdims=True)
        out_ref[block, 1, pl.ds(j, 1), :] = jnp.sum(accs[1], axis=0, keepdims=True)

    zero = jnp.zeros((8, 128), jnp.float32)

    def per_block_narrow(k, carry):
        block = meta_ref[1 + k]

        def per_panel(j, carry):
            slot = block * panels + j
            centre_row = pos_ref[2 * slot]
            centre_col = pos_ref[2 * slot + 1]
            first_row, _ = window(centre_row, row_base, reach_row, rows, 8)
            first_col, _ = window(centre_col, col_base, reach_col, cols, 128)
            first_row = jnp.minimum(first_row, row_tiles - 2)
            first_col = jnp.minimum(first_col, col_tiles - 2)
            accs = (zero, zero)
            for r in range(2):
                for c in range(2):
                    accs = tile_sums(centre_row, centre_col, first_row + r, first_col + c, accs)
            store(block, j, accs)
            return carry

        return lax.fori_loop(0, panels, per_panel, carry, unroll=4)

    def per_block_wide(k, carry):
        block = meta_ref[1 + k]

        def per_panel(j, carry):
            slot = block * panels + j
            centre_row = pos_ref[2 * slot]
            centre_col = pos_ref[2 * slot + 1]
            first_row, row_groups = window(centre_row, row_base, reach_row, rows, 8)
            first_col, col_groups = window(centre_col, col_base, reach_col, cols, 128)

            def per_row(r, accs):
                def per_col(c, accs):
                    return tile_sums(centre_row, centre_col, first_row + r, first_col + c, accs)

                return lax.fori_loop(0, col_groups, per_col, accs)

            store(block, j, lax.fori_loop(0, row_groups, per_row, (zero, zero)))
            return carry

        return lax.fori_loop(0, panels, per_panel, carry)

    narrow = (reach_row < 4.0) & (reach_col < 4.0)

    @pl.when(narrow)
    def _():
        lax.fori_loop(0, meta_ref[0], per_block_narrow, 0)

    @pl.when(jnp.logical_not(narrow))
    def _():
        lax.fori_loop(0, meta_ref[0], per_block_wide, 0)


def contact_sums(meta, geometry, positions, rows_x, cols_x):
    blocks = meta.shape[0] - 1
    smem = pl.BlockSpec(memory_space=pltpu.SMEM)
    vmem = pl.BlockSpec(memory_space=pltpu.VMEM)
    return pl.pallas_call(
        contact_kernel,
        out_shape=jax.ShapeDtypeStruct((blocks, 2, PAN_DEV, 128), jnp.float32),
        in_specs=[smem, smem, smem, vmem, vmem],
        out_specs=vmem,
    )(meta, geometry, positions, rows_x, cols_x)


def with_halo(block, sides, width):
    for axis, dim in sides:
        count = lax.axis_size(axis)
        forward = [(i, i + 1) for i in range(count - 1)]
        backward = [(target, source) for source, target in forward]
        narrow = dim == block.ndim - 1
        low = lax.slice_in_dim(block, block.shape[dim] - width, None, axis=dim)
        high = lax.slice_in_dim(block, 0, width, axis=dim)
        strip = low.shape
        if narrow:
            low, high = low.reshape(-1), high.reshape(-1)
        low = lax.ppermute(low, axis, forward).reshape(strip)
        high = lax.ppermute(high, axis, backward).reshape(strip)
        block = jnp.concatenate([low, block, high], axis=dim)
    return block


def forces(padded, bits, present_pad, rows, cols):
    centre = padded[:, 3 : 3 + rows, 3 : 3 + cols]
    total_row = jnp.zeros((rows, cols), jnp.float32)
    total_col = jnp.zeros((rows, cols), jnp.float32)
    kept_sum = jnp.zeros((rows, cols), jnp.float32)
    exist_sum = jnp.zeros((rows, cols), jnp.float32)
    for index, (row_off, col_off) in enumerate(offsets):
        other = padded[:, 3 + row_off : 3 + row_off + rows, 3 + col_off : 3 + col_off + cols]
        present = present_pad[3 + row_off : 3 + row_off + rows, 3 + col_off : 3 + col_off + cols]
        flag = jnp.bitwise_and(jnp.right_shift(bits[index // 14], index % 14), 1).astype(
            jnp.float32
        )
        keep = flag * present
        row_part = row_off + (other[0] - centre[0])
        col_part = col_off + (other[1] - centre[1])
        length = jnp.sqrt(row_part * row_part + col_part * col_part)
        rest = float((row_off * row_off + col_off * col_off) ** 0.5)
        coeff = keep * (length - rest) / (rest * length)
        total_row = total_row + coeff * row_part
        total_col = total_col + coeff * col_part
        kept_sum = kept_sum + keep
        exist_sum = exist_sum + present
    return (jnp.stack([total_row, total_col]), kept_sum, exist_sum)


def body(disp, velocity, bond_bits, panel_pos, contact_list):
    rows, cols = (disp.shape[1], disp.shape[2])
    along_count = lax.axis_size("along")
    across_count = lax.axis_size("across")
    total_rows = rows * along_count
    total_cols = cols * across_count
    row_base = lax.axis_index("along") * rows
    col_base = lax.axis_index("across") * cols
    stacked = jnp.concatenate([disp, velocity, bond_bits.astype(jnp.float32)], axis=0)
    ext = with_halo(stacked, (("along", 1), ("across", 2)), 6)
    grid_row = row_base - 6 + jnp.arange(rows + 12, dtype=jnp.int32)
    grid_col = col_base - 6 + jnp.arange(cols + 12, dtype=jnp.int32)
    inside_row = (grid_row >= 0) & (grid_row < total_rows)
    inside_col = (grid_col >= 0) & (grid_col < total_cols)
    present_wide = (inside_row[:, None] & inside_col[None, :]).astype(jnp.float32)
    present_ring = present_wide[3:-3, 3:-3]
    force, kept_sum, exist_sum = forces(
        ext[0:2], ext[4:6, 3:-3, 3:-3].astype(jnp.int32), present_wide, rows + 6, cols + 6
    )
    damage = 1.0 - kept_sum[3:-3, 3:-3] / exist_sum[3:-3, 3:-3]
    ring_v = ext[2:4, 3:-3, 3:-3] + 10.0 * force
    ring_u = ext[0:2, 3:-3, 3:-3] + 0.05 * ring_v
    ring_u = jnp.where(present_ring[None] > 0.0, ring_u, 0.0)
    force, _, _ = forces(ring_u, bond_bits, present_ring, rows, cols)
    state_v = ring_v[:, 3:-3, 3:-3] + 10.0 * force
    state_u = ring_u[:, 3:-3, 3:-3] + 0.05 * state_v
    block_count = lax.axis_size("along")
    packed = jnp.concatenate(
        [panel_pos.reshape(1, -1), contact_list.astype(jnp.float32).reshape(1, -1)], axis=1
    )
    gathered = lax.all_to_all(
        jnp.broadcast_to(packed[None], (block_count,) + packed.shape), "along", 0, 0, tiled=True
    ).reshape(block_count, -1)
    all_pos = gathered[:, : 2 * PAN_DEV].reshape(block_count, PAN_DEV, 2)
    all_lists = gathered[:, 2 * PAN_DEV :].astype(jnp.int32)
    my_tile = lax.axis_index("along") * across_count + lax.axis_index("across")
    listed = jnp.any(all_lists == my_tile, axis=1).astype(jnp.int32)
    prefix = jnp.cumsum(listed)
    n_listed = prefix[-1]
    slots = jnp.arange(block_count, dtype=jnp.int32)
    listed_blocks = jnp.sum((prefix[None, :] <= slots[:, None]).astype(jnp.int32), axis=1)
    rows_x = (row_base + jnp.arange(rows, dtype=jnp.int32)).astype(jnp.float32)[:, None] + state_u[0]
    cols_x = (col_base + jnp.arange(cols, dtype=jnp.int32)).astype(jnp.float32)[None, :] + state_u[1]
    reach_row = 2.5 + jnp.max(jnp.abs(state_u[0]))
    reach_col = 2.5 + jnp.max(jnp.abs(state_u[1]))
    geometry = jnp.stack(
        [reach_row, reach_col, row_base.astype(jnp.float32), col_base.astype(jnp.float32)]
    )
    meta = jnp.concatenate([n_listed[None], listed_blocks])
    sums = contact_sums(meta, geometry, all_pos.reshape(-1), rows_x, cols_x)
    partials = jnp.transpose(jnp.sum(sums, axis=-1), (0, 2, 1))
    spread = jnp.broadcast_to(
        partials.reshape(block_count, 1, 1, 2 * PAN_DEV),
        (block_count, across_count, 1, 2 * PAN_DEV),
    ).reshape(block_count * across_count, 1, 2 * PAN_DEV)
    arrived = lax.all_to_all(spread, ("along", "across"), 0, 0, tiled=True)
    panel_force = jnp.sum(arrived, axis=0).reshape(PAN_DEV, 2)
    return (state_u, state_v, damage, panel_force)


def solution(mesh):
    return jax.shard_map(
        body,
        mesh=mesh,
        in_specs=(
            P(None, "along", "across"),
            P(None, "along", "across"),
            P(None, "along", "across"),
            P("along", None),
            P("along", None),
        ),
        out_specs=(
            P(None, "along", "across"),
            P(None, "along", "across"),
            P("along", "across"),
            P("along", None),
        ),
        check_vma=False,
    )
```

```python
import jax
import jax.numpy as jnp
from jax import lax
from jax.experimental import pallas as pl
from jax.experimental.pallas import tpu as pltpu
from jax.sharding import PartitionSpec as P

PAN_DEV = 64


offsets = [(rr, cc) for rr in range(-3, 4) for cc in range(-3, 4) if 0 < rr * rr + cc * cc <= 9]


def contact_kernel(meta_ref, geo_ref, pos_ref, xr_ref, xc_ref, out_ref):
    out_ref[...] = jnp.zeros_like(out_ref)
    blocks, _, panels, _ = out_ref.shape
    rows, cols = xr_ref.shape
    row_tiles = rows // 8
    col_tiles = cols // 128
    reach_row, reach_col = geo_ref[0], geo_ref[1]
    row_base, col_base = geo_ref[2], geo_ref[3]

    def window(centre, base, reach, size, group):
        local = centre - base
        low = jnp.clip((local - reach).astype(jnp.int32), 0, size)
        high = jnp.clip((local + reach).astype(jnp.int32) + 1, 0, size)
        first = low // group
        return first, jnp.maximum((high + group - 1) // group - first, 0)

    def tile_sums(centre_row, centre_col, row_group, col_group, accs):
        row = pl.multiple_of(row_group * 8, 8)
        col = pl.multiple_of(col_group * 128, 128)
        delta_row = centre_row - xr_ref[pl.ds(row, 8), pl.ds(col, 128)]
        delta_col = centre_col - xc_ref[pl.ds(row, 8), pl.ds(col, 128)]
        push = 0.5 * jnp.maximum(4.0 - delta_row * delta_row - delta_col * delta_col, 0.0)
        return (accs[0] + push * delta_row, accs[1] + push * delta_col)

    def store(block, j, accs):
        out_ref[block, 0, pl.ds(j, 1), :] = jnp.sum(accs[0], axis=0, keepdims=True)
        out_ref[block, 1, pl.ds(j, 1), :] = jnp.sum(accs[1], axis=0, keepdims=True)

    zero = jnp.zeros((8, 128), jnp.float32)

    def per_block_narrow(k, carry):
        block = meta_ref[1 + k]

        def per_panel(j, carry):
            slot = block * panels + j
            centre_row = pos_ref[2 * slot]
            centre_col = pos_ref[2 * slot + 1]
            first_row, _ = window(centre_row, row_base, reach_row, rows, 8)
            first_col, _ = window(centre_col, col_base, reach_col, cols, 128)
            first_row = jnp.minimum(first_row, row_tiles - 2)
            first_col = jnp.minimum(first_col, col_tiles - 2)
            accs = (zero, zero)
            for r in range(2):
                for c in range(2):
                    accs = tile_sums(centre_row, centre_col, first_row + r, first_col + c, accs)
            store(block, j, accs)
            return carry

        return lax.fori_loop(0, panels, per_panel, carry, unroll=4)

    def per_block_wide(k, carry):
        block = meta_ref[1 + k]

        def per_panel(j, carry):
            slot = block * panels + j
            centre_row = pos_ref[2 * slot]
            centre_col = pos_ref[2 * slot + 1]
            first_row, row_groups = window(centre_row, row_base, reach_row, rows, 8)
            first_col, col_groups = window(centre_col, col_base, reach_col, cols, 128)

            def per_row(r, accs):
                def per_col(c, accs):
                    return tile_sums(centre_row, centre_col, first_row + r, first_col + c, accs)

                return lax.fori_loop(0, col_groups, per_col, accs)

            store(block, j, lax.fori_loop(0, row_groups, per_row, (zero, zero)))
            return carry

        return lax.fori_loop(0, panels, per_panel, carry)

    narrow = (reach_row < 4.0) & (reach_col < 4.0)

    @pl.when(narrow)
    def _():
        lax.fori_loop(0, meta_ref[0], per_block_narrow, 0)

    @pl.when(jnp.logical_not(narrow))
    def _():
        lax.fori_loop(0, meta_ref[0], per_block_wide, 0)


def contact_sums(meta, geometry, positions, rows_x, cols_x):
    blocks = meta.shape[0] - 1
    smem = pl.BlockSpec(memory_space=pltpu.SMEM)
    vmem = pl.BlockSpec(memory_space=pltpu.VMEM)
    return pl.pallas_call(
        contact_kernel,
        out_shape=jax.ShapeDtypeStruct((blocks, 2, PAN_DEV, 128), jnp.float32),
        in_specs=[smem, smem, smem, vmem, vmem],
        out_specs=vmem,
    )(meta, geometry, positions, rows_x, cols_x)


def with_halo(block, sides, width):
    for axis, dim in sides:
        count = lax.axis_size(axis)
        forward = [(i, i + 1) for i in range(count - 1)]
        backward = [(target, source) for source, target in forward]
        narrow = dim == block.ndim - 1
        low = lax.slice_in_dim(block, block.shape[dim] - width, None, axis=dim)
        high = lax.slice_in_dim(block, 0, width, axis=dim)
        strip = low.shape
        if narrow:
            low, high = low.reshape(-1), high.reshape(-1)
        low = lax.ppermute(low, axis, forward).reshape(strip)
        high = lax.ppermute(high, axis, backward).reshape(strip)
        block = jnp.concatenate([low, block, high], axis=dim)
    return block


def bond_counts(bits, present_pad, rows, cols):
    kept_sum = jnp.zeros((rows, cols), jnp.float32)
    exist_sum = jnp.zeros((rows, cols), jnp.float32)
    for index, (row_off, col_off) in enumerate(offsets):
        present = present_pad[3 + row_off : 3 + row_off + rows, 3 + col_off : 3 + col_off + cols]
        flag = jnp.bitwise_and(jnp.right_shift(bits[index // 14], index % 14), 1).astype(
            jnp.float32
        )
        kept_sum = kept_sum + flag * present
        exist_sum = exist_sum + present
    return kept_sum, exist_sum


def forces(padded, bits, present_pad, rows, cols):
    centre = padded[:, 3 : 3 + rows, 3 : 3 + cols]
    total_row = jnp.zeros((rows, cols), jnp.float32)
    total_col = jnp.zeros((rows, cols), jnp.float32)
    kept_sum = jnp.zeros((rows, cols), jnp.float32)
    exist_sum = jnp.zeros((rows, cols), jnp.float32)
    for index, (row_off, col_off) in enumerate(offsets):
        other = padded[:, 3 + row_off : 3 + row_off + rows, 3 + col_off : 3 + col_off + cols]
        present = present_pad[3 + row_off : 3 + row_off + rows, 3 + col_off : 3 + col_off + cols]
        flag = jnp.bitwise_and(jnp.right_shift(bits[index // 14], index % 14), 1).astype(
            jnp.float32
        )
        keep = flag * present
        row_part = row_off + (other[0] - centre[0])
        col_part = col_off + (other[1] - centre[1])
        length = jnp.sqrt(row_part * row_part + col_part * col_part)
        rest = float((row_off * row_off + col_off * col_off) ** 0.5)
        coeff = keep * (length - rest) / (rest * length)
        total_row = total_row + coeff * row_part
        total_col = total_col + coeff * col_part
        kept_sum = kept_sum + keep
        exist_sum = exist_sum + present
    return (jnp.stack([total_row, total_col]), kept_sum, exist_sum)


def body(disp, velocity, bond_bits, panel_pos, contact_list):
    rows, cols = (disp.shape[1], disp.shape[2])
    along_count = lax.axis_size("along")
    across_count = lax.axis_size("across")
    total_rows = rows * along_count
    total_cols = cols * across_count
    row_base = lax.axis_index("along") * rows
    col_base = lax.axis_index("across") * cols
    stacked = jnp.concatenate([disp, velocity, bond_bits.astype(jnp.float32)], axis=0)
    ext = with_halo(stacked, (("along", 1), ("across", 2)), 6)
    grid_row = row_base - 6 + jnp.arange(rows + 12, dtype=jnp.int32)
    grid_col = col_base - 6 + jnp.arange(cols + 12, dtype=jnp.int32)
    inside_row = (grid_row >= 0) & (grid_row < total_rows)
    inside_col = (grid_col >= 0) & (grid_col < total_cols)
    present_wide = (inside_row[:, None] & inside_col[None, :]).astype(jnp.float32)
    present_ring = present_wide[3:-3, 3:-3]
    force, _, _ = forces(
        ext[0:2], ext[4:6, 3:-3, 3:-3].astype(jnp.int32), present_wide, rows + 6, cols + 6
    )
    kept_sum, exist_sum = bond_counts(bond_bits, present_ring, rows, cols)
    damage = 1.0 - kept_sum / exist_sum
    ring_v = ext[2:4, 3:-3, 3:-3] + 10.0 * force
    ring_u = ext[0:2, 3:-3, 3:-3] + 0.05 * ring_v
    ring_u = jnp.where(present_ring[None] > 0.0, ring_u, 0.0)
    force, _, _ = forces(ring_u, bond_bits, present_ring, rows, cols)
    state_v = ring_v[:, 3:-3, 3:-3] + 10.0 * force
    state_u = ring_u[:, 3:-3, 3:-3] + 0.05 * state_v
    block_count = lax.axis_size("along")
    packed = jnp.concatenate(
        [panel_pos.reshape(1, -1), contact_list.astype(jnp.float32).reshape(1, -1)], axis=1
    )
    gathered = lax.all_to_all(
        jnp.broadcast_to(packed[None], (block_count,) + packed.shape), "along", 0, 0, tiled=True
    ).reshape(block_count, -1)
    all_pos = gathered[:, : 2 * PAN_DEV].reshape(block_count, PAN_DEV, 2)
    all_lists = gathered[:, 2 * PAN_DEV :].astype(jnp.int32)
    my_tile = lax.axis_index("along") * across_count + lax.axis_index("across")
    listed = jnp.any(all_lists == my_tile, axis=1).astype(jnp.int32)
    prefix = jnp.cumsum(listed)
    n_listed = prefix[-1]
    slots = jnp.arange(block_count, dtype=jnp.int32)
    listed_blocks = jnp.sum((prefix[None, :] <= slots[:, None]).astype(jnp.int32), axis=1)
    rows_x = (row_base + jnp.arange(rows, dtype=jnp.int32)).astype(jnp.float32)[:, None] + state_u[0]
    cols_x = (col_base + jnp.arange(cols, dtype=jnp.int32)).astype(jnp.float32)[None, :] + state_u[1]
    reach_row = 2.5 + jnp.max(jnp.abs(state_u[0]))
    reach_col = 2.5 + jnp.max(jnp.abs(state_u[1]))
    geometry = jnp.stack(
        [reach_row, reach_col, row_base.astype(jnp.float32), col_base.astype(jnp.float32)]
    )
    meta = jnp.concatenate([n_listed[None], listed_blocks])
    sums = contact_sums(meta, geometry, all_pos.reshape(-1), rows_x, cols_x)
    partials = jnp.transpose(jnp.sum(sums, axis=-1), (0, 2, 1))
    spread = jnp.broadcast_to(
        partials.reshape(block_count, 1, 1, 2 * PAN_DEV),
        (block_count, across_count, 1, 2 * PAN_DEV),
    ).reshape(block_count * across_count, 1, 2 * PAN_DEV)
    arrived = lax.all_to_all(spread, ("along", "across"), 0, 0, tiled=True)
    panel_force = jnp.sum(arrived, axis=0).reshape(PAN_DEV, 2)
    return (state_u, state_v, damage, panel_force)


def solution(mesh):
    return jax.shard_map(
        body,
        mesh=mesh,
        in_specs=(
            P(None, "along", "across"),
            P(None, "along", "across"),
            P(None, "along", "across"),
            P("along", None),
            P("along", None),
        ),
        out_specs=(
            P(None, "along", "across"),
            P(None, "along", "across"),
            P("along", "across"),
            P("along", None),
        ),
        check_vma=False,
    )
```

```python
import jax
import jax.numpy as jnp
from jax import lax
from jax.experimental import pallas as pl
from jax.experimental.pallas import tpu as pltpu
from jax.sharding import PartitionSpec as P

PAN_DEV = 64


offsets = [(rr, cc) for rr in range(-3, 4) for cc in range(-3, 4) if 0 < rr * rr + cc * cc <= 9]


def contact_kernel(meta_ref, geo_ref, pos_ref, xr_ref, xc_ref, out_ref):
    out_ref[...] = jnp.zeros_like(out_ref)
    blocks, _, panels, _ = out_ref.shape
    rows, cols = xr_ref.shape
    row_tiles = rows // 8
    col_tiles = cols // 128
    reach_row, reach_col = geo_ref[0], geo_ref[1]
    row_base, col_base = geo_ref[2], geo_ref[3]

    def window(centre, base, reach, size, group):
        local = centre - base
        low = jnp.clip((local - reach).astype(jnp.int32), 0, size)
        high = jnp.clip((local + reach).astype(jnp.int32) + 1, 0, size)
        first = low // group
        return first, jnp.maximum((high + group - 1) // group - first, 0)

    def tile_sums(centre_row, centre_col, row_group, col_group, accs):
        row = pl.multiple_of(row_group * 8, 8)
        col = pl.multiple_of(col_group * 128, 128)
        delta_row = centre_row - xr_ref[pl.ds(row, 8), pl.ds(col, 128)]
        delta_col = centre_col - xc_ref[pl.ds(row, 8), pl.ds(col, 128)]
        push = 0.5 * jnp.maximum(4.0 - delta_row * delta_row - delta_col * delta_col, 0.0)
        return (accs[0] + push * delta_row, accs[1] + push * delta_col)

    def store(block, j, accs):
        out_ref[block, 0, pl.ds(j, 1), :] = jnp.sum(accs[0], axis=0, keepdims=True)
        out_ref[block, 1, pl.ds(j, 1), :] = jnp.sum(accs[1], axis=0, keepdims=True)

    zero = jnp.zeros((8, 128), jnp.float32)

    def per_block_narrow(k, carry):
        block = meta_ref[1 + k]

        def per_panel(j, carry):
            slot = block * panels + j
            centre_row = pos_ref[2 * slot]
            centre_col = pos_ref[2 * slot + 1]
            first_row, _ = window(centre_row, row_base, reach_row, rows, 8)
            first_col, _ = window(centre_col, col_base, reach_col, cols, 128)
            first_row = jnp.minimum(first_row, row_tiles - 2)
            first_col = jnp.minimum(first_col, col_tiles - 2)
            accs = (zero, zero)
            for r in range(2):
                for c in range(2):
                    accs = tile_sums(centre_row, centre_col, first_row + r, first_col + c, accs)
            store(block, j, accs)
            return carry

        return lax.fori_loop(0, panels, per_panel, carry, unroll=4)

    def per_block_wide(k, carry):
        block = meta_ref[1 + k]

        def per_panel(j, carry):
            slot = block * panels + j
            centre_row = pos_ref[2 * slot]
            centre_col = pos_ref[2 * slot + 1]
            first_row, row_groups = window(centre_row, row_base, reach_row, rows, 8)
            first_col, col_groups = window(centre_col, col_base, reach_col, cols, 128)

            def per_row(r, accs):
                def per_col(c, accs):
                    return tile_sums(centre_row, centre_col, first_row + r, first_col + c, accs)

                return lax.fori_loop(0, col_groups, per_col, accs)

            store(block, j, lax.fori_loop(0, row_groups, per_row, (zero, zero)))
            return carry

        return lax.fori_loop(0, panels, per_panel, carry)

    narrow = (reach_row < 4.0) & (reach_col < 4.0)

    @pl.when(narrow)
    def _():
        lax.fori_loop(0, meta_ref[0], per_block_narrow, 0)

    @pl.when(jnp.logical_not(narrow))
    def _():
        lax.fori_loop(0, meta_ref[0], per_block_wide, 0)


def contact_sums(meta, geometry, positions, rows_x, cols_x):
    blocks = meta.shape[0] - 1
    smem = pl.BlockSpec(memory_space=pltpu.SMEM)
    vmem = pl.BlockSpec(memory_space=pltpu.VMEM)
    return pl.pallas_call(
        contact_kernel,
        out_shape=jax.ShapeDtypeStruct((blocks, 2, PAN_DEV, 128), jnp.float32),
        in_specs=[smem, smem, smem, vmem, vmem],
        out_specs=vmem,
    )(meta, geometry, positions, rows_x, cols_x)


def with_halo(block, sides, width):
    for axis, dim in sides:
        count = lax.axis_size(axis)
        forward = [(i, i + 1) for i in range(count - 1)]
        backward = [(target, source) for source, target in forward]
        narrow = dim == block.ndim - 1
        low = lax.slice_in_dim(block, block.shape[dim] - width, None, axis=dim)
        high = lax.slice_in_dim(block, 0, width, axis=dim)
        strip = low.shape
        if narrow:
            low, high = low.reshape(-1), high.reshape(-1)
        low = lax.ppermute(low, axis, forward).reshape(strip)
        high = lax.ppermute(high, axis, backward).reshape(strip)
        block = jnp.concatenate([low, block, high], axis=dim)
    return block


def bond_counts(bits, present_pad, rows, cols):
    kept_sum = jnp.zeros((rows, cols), jnp.float32)
    exist_sum = jnp.zeros((rows, cols), jnp.float32)
    for index, (row_off, col_off) in enumerate(offsets):
        present = present_pad[3 + row_off : 3 + row_off + rows, 3 + col_off : 3 + col_off + cols]
        flag = jnp.bitwise_and(jnp.right_shift(bits[index // 14], index % 14), 1).astype(
            jnp.float32
        )
        kept_sum = kept_sum + flag * present
        exist_sum = exist_sum + present
    return kept_sum, exist_sum


def forces(padded, bits, present_pad, rows, cols):
    centre = padded[:, 3 : 3 + rows, 3 : 3 + cols]
    total_row = jnp.zeros((rows, cols), jnp.float32)
    total_col = jnp.zeros((rows, cols), jnp.float32)
    kept_sum = jnp.zeros((rows, cols), jnp.float32)
    exist_sum = jnp.zeros((rows, cols), jnp.float32)
    for index, (row_off, col_off) in enumerate(offsets):
        other = padded[:, 3 + row_off : 3 + row_off + rows, 3 + col_off : 3 + col_off + cols]
        present = present_pad[3 + row_off : 3 + row_off + rows, 3 + col_off : 3 + col_off + cols]
        flag = jnp.bitwise_and(jnp.right_shift(bits[index // 14], index % 14), 1).astype(
            jnp.float32
        )
        keep = flag * present
        row_part = row_off + (other[0] - centre[0])
        col_part = col_off + (other[1] - centre[1])
        length = jnp.sqrt(row_part * row_part + col_part * col_part)
        rest = float((row_off * row_off + col_off * col_off) ** 0.5)
        coeff = keep * (length - rest) / (rest * length)
        total_row = total_row + coeff * row_part
        total_col = total_col + coeff * col_part
        kept_sum = kept_sum + keep
        exist_sum = exist_sum + present
    return (jnp.stack([total_row, total_col]), kept_sum, exist_sum)


def body(disp, velocity, bond_bits, panel_pos, contact_list):
    rows, cols = (disp.shape[1], disp.shape[2])
    along_count = lax.axis_size("along")
    across_count = lax.axis_size("across")
    total_rows = rows * along_count
    total_cols = cols * across_count
    row_base = lax.axis_index("along") * rows
    col_base = lax.axis_index("across") * cols
    stacked = jnp.concatenate([disp, velocity, bond_bits.astype(jnp.float32)], axis=0)
    ext = with_halo(stacked, (("along", 1), ("across", 2)), 6)
    grid_row = row_base - 6 + jnp.arange(rows + 12, dtype=jnp.int32)
    grid_col = col_base - 6 + jnp.arange(cols + 12, dtype=jnp.int32)
    inside_row = (grid_row >= 0) & (grid_row < total_rows)
    inside_col = (grid_col >= 0) & (grid_col < total_cols)
    present_wide = (inside_row[:, None] & inside_col[None, :]).astype(jnp.float32)
    present_ring = present_wide[3:-3, 3:-3]
    force, _, _ = forces(
        ext[0:2], ext[4:6, 3:-3, 3:-3].astype(jnp.int32), present_wide, rows + 6, cols + 6
    )
    kept_sum, exist_sum = bond_counts(bond_bits, present_ring, rows, cols)
    damage = 1.0 - kept_sum / exist_sum
    ring_v = ext[2:4, 3:-3, 3:-3] + 10.0 * force
    ring_u = ext[0:2, 3:-3, 3:-3] + 0.05 * ring_v
    ring_u = jnp.where(present_ring[None] > 0.0, ring_u, 0.0)
    force, _, _ = forces(ring_u, bond_bits, present_ring, rows, cols)
    state_v = ring_v[:, 3:-3, 3:-3] + 10.0 * force
    state_u = ring_u[:, 3:-3, 3:-3] + 0.05 * state_v
    block_count = lax.axis_size("along")
    packed = jnp.concatenate(
        [panel_pos.reshape(1, -1), contact_list.astype(jnp.float32).reshape(1, -1)], axis=1
    )
    gathered = lax.all_to_all(
        jnp.broadcast_to(packed[None], (block_count,) + packed.shape), "along", 0, 0, tiled=True
    ).reshape(block_count, -1)
    gathered, state_u = lax.optimization_barrier((gathered, state_u))
    all_pos = gathered[:, : 2 * PAN_DEV].reshape(block_count, PAN_DEV, 2)
    all_lists = gathered[:, 2 * PAN_DEV :].astype(jnp.int32)
    my_tile = lax.axis_index("along") * across_count + lax.axis_index("across")
    listed = jnp.any(all_lists == my_tile, axis=1).astype(jnp.int32)
    prefix = jnp.cumsum(listed)
    n_listed = prefix[-1]
    slots = jnp.arange(block_count, dtype=jnp.int32)
    listed_blocks = jnp.sum((prefix[None, :] <= slots[:, None]).astype(jnp.int32), axis=1)
    rows_x = (row_base + jnp.arange(rows, dtype=jnp.int32)).astype(jnp.float32)[:, None] + state_u[0]
    cols_x = (col_base + jnp.arange(cols, dtype=jnp.int32)).astype(jnp.float32)[None, :] + state_u[1]
    reach_row = 2.5 + jnp.max(jnp.abs(state_u[0]))
    reach_col = 2.5 + jnp.max(jnp.abs(state_u[1]))
    geometry = jnp.stack(
        [reach_row, reach_col, row_base.astype(jnp.float32), col_base.astype(jnp.float32)]
    )
    meta = jnp.concatenate([n_listed[None], listed_blocks])
    sums = contact_sums(meta, geometry, all_pos.reshape(-1), rows_x, cols_x)
    partials = jnp.transpose(jnp.sum(sums, axis=-1), (0, 2, 1))
    spread = jnp.broadcast_to(
        partials.reshape(block_count, 1, 1, 2 * PAN_DEV),
        (block_count, across_count, 1, 2 * PAN_DEV),
    ).reshape(block_count * across_count, 1, 2 * PAN_DEV)
    arrived = lax.all_to_all(spread, ("along", "across"), 0, 0, tiled=True)
    panel_force = jnp.sum(arrived, axis=0).reshape(PAN_DEV, 2)
    return (state_u, state_v, damage, panel_force)


def solution(mesh):
    return jax.shard_map(
        body,
        mesh=mesh,
        in_specs=(
            P(None, "along", "across"),
            P(None, "along", "across"),
            P(None, "along", "across"),
            P("along", None),
            P("along", None),
        ),
        out_specs=(
            P(None, "along", "across"),
            P(None, "along", "across"),
            P("along", "across"),
            P("along", None),
        ),
        check_vma=False,
    )
```

```python
import jax
import jax.numpy as jnp
from jax import lax
from jax.experimental import pallas as pl
from jax.experimental.pallas import tpu as pltpu
from jax.sharding import PartitionSpec as P

PAN_DEV = 64


offsets = [(rr, cc) for rr in range(-3, 4) for cc in range(-3, 4) if 0 < rr * rr + cc * cc <= 9]


def contact_kernel(geo_ref, pos_ref, xr_ref, xc_ref, out_ref):
    out_ref[...] = jnp.zeros_like(out_ref)
    blocks, _, panels, _ = out_ref.shape
    rows, cols = xr_ref.shape
    row_tiles = rows // 8
    col_tiles = cols // 128
    reach_row, reach_col = geo_ref[0], geo_ref[1]
    row_base, col_base, my_tile = geo_ref[2], geo_ref[3], geo_ref[4]
    stride = pos_ref.shape[0] // blocks
    listing = stride - 2 * panels

    def window(centre, base, reach, size, group):
        local = centre - base
        low = jnp.clip((local - reach).astype(jnp.int32), 0, size)
        high = jnp.clip((local + reach).astype(jnp.int32) + 1, 0, size)
        first = low // group
        return first, jnp.maximum((high + group - 1) // group - first, 0)

    def tile_sums(centre_row, centre_col, row_group, col_group, accs):
        row = pl.multiple_of(row_group * 8, 8)
        col = pl.multiple_of(col_group * 128, 128)
        delta_row = centre_row - xr_ref[pl.ds(row, 8), pl.ds(col, 128)]
        delta_col = centre_col - xc_ref[pl.ds(row, 8), pl.ds(col, 128)]
        push = 0.5 * jnp.maximum(4.0 - delta_row * delta_row - delta_col * delta_col, 0.0)
        return (accs[0] + push * delta_row, accs[1] + push * delta_col)

    def store(block, j, accs):
        out_ref[block, 0, pl.ds(j, 1), :] = jnp.sum(accs[0], axis=0, keepdims=True)
        out_ref[block, 1, pl.ds(j, 1), :] = jnp.sum(accs[1], axis=0, keepdims=True)

    zero = jnp.zeros((8, 128), jnp.float32)

    def per_block_narrow(block):
        def per_panel(j, carry):
            centre_row = pos_ref[block * stride + 2 * j]
            centre_col = pos_ref[block * stride + 2 * j + 1]
            first_row, _ = window(centre_row, row_base, reach_row, rows, 8)
            first_col, _ = window(centre_col, col_base, reach_col, cols, 128)
            first_row = jnp.minimum(first_row, row_tiles - 2)
            first_col = jnp.minimum(first_col, col_tiles - 2)
            accs = (zero, zero)
            for r in range(2):
                for c in range(2):
                    accs = tile_sums(centre_row, centre_col, first_row + r, first_col + c, accs)
            store(block, j, accs)
            return carry

        lax.fori_loop(0, panels, per_panel, 0, unroll=8)

    def per_block_wide(block):
        def per_panel(j, carry):
            centre_row = pos_ref[block * stride + 2 * j]
            centre_col = pos_ref[block * stride + 2 * j + 1]
            first_row, row_groups = window(centre_row, row_base, reach_row, rows, 8)
            first_col, col_groups = window(centre_col, col_base, reach_col, cols, 128)

            def per_row(r, accs):
                def per_col(c, accs):
                    return tile_sums(centre_row, centre_col, first_row + r, first_col + c, accs)

                return lax.fori_loop(0, col_groups, per_col, accs)

            store(block, j, lax.fori_loop(0, row_groups, per_row, (zero, zero)))
            return carry

        lax.fori_loop(0, panels, per_panel, 0)

    narrow = (reach_row < 4.0) & (reach_col < 4.0)

    def per_block(block, carry):
        listed = pos_ref[block * stride + 2 * panels] == my_tile
        for slot in range(1, listing):
            listed = listed | (pos_ref[block * stride + 2 * panels + slot] == my_tile)

        @pl.when(listed & narrow)
        def _():
            per_block_narrow(block)

        @pl.when(listed & jnp.logical_not(narrow))
        def _():
            per_block_wide(block)

        return carry

    lax.fori_loop(0, blocks, per_block, 0)


def contact_sums(geometry, gathered, rows_x, cols_x):
    blocks = gathered.shape[0]
    smem = pl.BlockSpec(memory_space=pltpu.SMEM)
    vmem = pl.BlockSpec(memory_space=pltpu.VMEM)
    return pl.pallas_call(
        contact_kernel,
        out_shape=jax.ShapeDtypeStruct((blocks, 2, PAN_DEV, 128), jnp.float32),
        in_specs=[smem, smem, vmem, vmem],
        out_specs=vmem,
    )(geometry, gathered.reshape(-1), rows_x, cols_x)


def with_halo(block, sides, width):
    for axis, dim in sides:
        count = lax.axis_size(axis)
        forward = [(i, i + 1) for i in range(count - 1)]
        backward = [(target, source) for source, target in forward]
        narrow = dim == block.ndim - 1
        low = lax.slice_in_dim(block, block.shape[dim] - width, None, axis=dim)
        high = lax.slice_in_dim(block, 0, width, axis=dim)
        strip = low.shape
        if narrow:
            low, high = low.reshape(-1), high.reshape(-1)
        low = lax.ppermute(low, axis, forward).reshape(strip)
        high = lax.ppermute(high, axis, backward).reshape(strip)
        block = jnp.concatenate([low, block, high], axis=dim)
    return block


def bond_counts(bits, present_pad, rows, cols):
    kept_sum = jnp.zeros((rows, cols), jnp.float32)
    exist_sum = jnp.zeros((rows, cols), jnp.float32)
    for index, (row_off, col_off) in enumerate(offsets):
        present = present_pad[3 + row_off : 3 + row_off + rows, 3 + col_off : 3 + col_off + cols]
        flag = jnp.bitwise_and(jnp.right_shift(bits[index // 14], index % 14), 1).astype(
            jnp.float32
        )
        kept_sum = kept_sum + flag * present
        exist_sum = exist_sum + present
    return kept_sum, exist_sum


def forces(padded, bits, present_pad, rows, cols):
    centre = padded[:, 3 : 3 + rows, 3 : 3 + cols]
    total_row = jnp.zeros((rows, cols), jnp.float32)
    total_col = jnp.zeros((rows, cols), jnp.float32)
    kept_sum = jnp.zeros((rows, cols), jnp.float32)
    exist_sum = jnp.zeros((rows, cols), jnp.float32)
    for index, (row_off, col_off) in enumerate(offsets):
        other = padded[:, 3 + row_off : 3 + row_off + rows, 3 + col_off : 3 + col_off + cols]
        present = present_pad[3 + row_off : 3 + row_off + rows, 3 + col_off : 3 + col_off + cols]
        flag = jnp.bitwise_and(jnp.right_shift(bits[index // 14], index % 14), 1).astype(
            jnp.float32
        )
        keep = flag * present
        row_part = row_off + (other[0] - centre[0])
        col_part = col_off + (other[1] - centre[1])
        length = jnp.sqrt(row_part * row_part + col_part * col_part)
        rest = float((row_off * row_off + col_off * col_off) ** 0.5)
        coeff = keep * (length - rest) / (rest * length)
        total_row = total_row + coeff * row_part
        total_col = total_col + coeff * col_part
        kept_sum = kept_sum + keep
        exist_sum = exist_sum + present
    return (jnp.stack([total_row, total_col]), kept_sum, exist_sum)


def body(disp, velocity, bond_bits, panel_pos, contact_list):
    rows, cols = (disp.shape[1], disp.shape[2])
    along_count = lax.axis_size("along")
    across_count = lax.axis_size("across")
    total_rows = rows * along_count
    total_cols = cols * across_count
    row_base = lax.axis_index("along") * rows
    col_base = lax.axis_index("across") * cols
    stacked = jnp.concatenate([disp, velocity, bond_bits.astype(jnp.float32)], axis=0)
    ext = with_halo(stacked, (("along", 1), ("across", 2)), 6)
    grid_row = row_base - 6 + jnp.arange(rows + 12, dtype=jnp.int32)
    grid_col = col_base - 6 + jnp.arange(cols + 12, dtype=jnp.int32)
    inside_row = (grid_row >= 0) & (grid_row < total_rows)
    inside_col = (grid_col >= 0) & (grid_col < total_cols)
    present_wide = (inside_row[:, None] & inside_col[None, :]).astype(jnp.float32)
    present_ring = present_wide[3:-3, 3:-3]
    force, _, _ = forces(
        ext[0:2], ext[4:6, 3:-3, 3:-3].astype(jnp.int32), present_wide, rows + 6, cols + 6
    )
    kept_sum, exist_sum = bond_counts(bond_bits, present_ring, rows, cols)
    damage = 1.0 - kept_sum / exist_sum
    ring_v = ext[2:4, 3:-3, 3:-3] + 10.0 * force
    ring_u = ext[0:2, 3:-3, 3:-3] + 0.05 * ring_v
    ring_u = jnp.where(present_ring[None] > 0.0, ring_u, 0.0)
    force, _, _ = forces(ring_u, bond_bits, present_ring, rows, cols)
    state_v = ring_v[:, 3:-3, 3:-3] + 10.0 * force
    state_u = ring_u[:, 3:-3, 3:-3] + 0.05 * state_v
    block_count = lax.axis_size("along")
    packed = jnp.concatenate(
        [panel_pos.reshape(1, -1), contact_list.astype(jnp.float32).reshape(1, -1)], axis=1
    )
    gathered = lax.all_to_all(
        jnp.broadcast_to(packed[None], (block_count,) + packed.shape), "along", 0, 0, tiled=True
    ).reshape(block_count, -1)
    gathered, state_u = lax.optimization_barrier((gathered, state_u))
    my_tile = lax.axis_index("along") * across_count + lax.axis_index("across")
    rows_x = (row_base + jnp.arange(rows, dtype=jnp.int32)).astype(jnp.float32)[:, None] + state_u[0]
    cols_x = (col_base + jnp.arange(cols, dtype=jnp.int32)).astype(jnp.float32)[None, :] + state_u[1]
    reach_row = 2.5 + jnp.max(jnp.abs(state_u[0]))
    reach_col = 2.5 + jnp.max(jnp.abs(state_u[1]))
    geometry = jnp.stack(
        [
            reach_row,
            reach_col,
            row_base.astype(jnp.float32),
            col_base.astype(jnp.float32),
            my_tile.astype(jnp.float32),
        ]
    )
    sums = contact_sums(geometry, gathered, rows_x, cols_x)
    partials = jnp.transpose(jnp.sum(sums, axis=-1), (0, 2, 1))
    spread = jnp.broadcast_to(
        partials.reshape(block_count, 1, 1, 2 * PAN_DEV),
        (block_count, across_count, 1, 2 * PAN_DEV),
    ).reshape(block_count * across_count, 1, 2 * PAN_DEV)
    arrived = lax.all_to_all(spread, ("along", "across"), 0, 0, tiled=True)
    panel_force = jnp.sum(arrived, axis=0).reshape(PAN_DEV, 2)
    return (state_u, state_v, damage, panel_force)


def solution(mesh):
    return jax.shard_map(
        body,
        mesh=mesh,
        in_specs=(
            P(None, "along", "across"),
            P(None, "along", "across"),
            P(None, "along", "across"),
            P("along", None),
            P("along", None),
        ),
        out_specs=(
            P(None, "along", "across"),
            P(None, "along", "across"),
            P("along", "across"),
            P("along", None),
        ),
        check_vma=False,
    )
```

```python
import jax
import jax.numpy as jnp
from jax import lax
from jax.experimental import pallas as pl
from jax.experimental.pallas import tpu as pltpu
from jax.sharding import PartitionSpec as P

PAN_DEV = 64


offsets = [(rr, cc) for rr in range(-3, 4) for cc in range(-3, 4) if 0 < rr * rr + cc * cc <= 9]


def contact_kernel(geo_ref, pos_ref, xr_ref, xc_ref, out_ref):
    out_ref[...] = jnp.zeros_like(out_ref)
    blocks, _, panels, _ = out_ref.shape
    rows, cols = xr_ref.shape
    row_tiles = rows // 8
    col_tiles = cols // 128
    reach_row, reach_col = geo_ref[0], geo_ref[1]
    row_base, col_base, my_tile = geo_ref[2], geo_ref[3], geo_ref[4]
    stride = pos_ref.shape[0] // blocks
    listing = stride - 2 * panels

    def window(centre, base, reach, size, group):
        local = centre - base
        low = jnp.clip((local - reach).astype(jnp.int32), 0, size)
        high = jnp.clip((local + reach).astype(jnp.int32) + 1, 0, size)
        first = low // group
        return first, jnp.maximum((high + group - 1) // group - first, 0)

    def tile_sums(centre_row, centre_col, row_group, col_group, accs):
        row = pl.multiple_of(row_group * 8, 8)
        col = pl.multiple_of(col_group * 128, 128)
        delta_row = centre_row - xr_ref[pl.ds(row, 8), pl.ds(col, 128)]
        delta_col = centre_col - xc_ref[pl.ds(row, 8), pl.ds(col, 128)]
        push = 0.5 * jnp.maximum(4.0 - delta_row * delta_row - delta_col * delta_col, 0.0)
        return (accs[0] + push * delta_row, accs[1] + push * delta_col)

    def store(block, j, accs):
        out_ref[block, 0, pl.ds(j, 1), :] = jnp.sum(accs[0], axis=0, keepdims=True)
        out_ref[block, 1, pl.ds(j, 1), :] = jnp.sum(accs[1], axis=0, keepdims=True)

    zero = jnp.zeros((8, 128), jnp.float32)

    def per_block_narrow(block):
        def per_panel(j, carry):
            centre_row = pos_ref[block * stride + 2 * j]
            centre_col = pos_ref[block * stride + 2 * j + 1]
            first_row, _ = window(centre_row, row_base, reach_row, rows, 8)
            first_col, _ = window(centre_col, col_base, reach_col, cols, 128)
            first_row = jnp.minimum(first_row, row_tiles - 2)
            first_col = jnp.minimum(first_col, col_tiles - 2)
            accs = (zero, zero)
            for r in range(2):
                for c in range(2):
                    accs = tile_sums(centre_row, centre_col, first_row + r, first_col + c, accs)
            store(block, j, accs)
            return carry

        lax.fori_loop(0, panels, per_panel, 0, unroll=8)

    def per_block_wide(block):
        def per_panel(j, carry):
            centre_row = pos_ref[block * stride + 2 * j]
            centre_col = pos_ref[block * stride + 2 * j + 1]
            first_row, row_groups = window(centre_row, row_base, reach_row, rows, 8)
            first_col, col_groups = window(centre_col, col_base, reach_col, cols, 128)

            def per_row(r, accs):
                def per_col(c, accs):
                    return tile_sums(centre_row, centre_col, first_row + r, first_col + c, accs)

                return lax.fori_loop(0, col_groups, per_col, accs)

            store(block, j, lax.fori_loop(0, row_groups, per_row, (zero, zero)))
            return carry

        lax.fori_loop(0, panels, per_panel, 0)

    narrow = (reach_row < 4.0) & (reach_col < 4.0)

    def per_block(block, carry):
        listed = pos_ref[block * stride + 2 * panels] == my_tile
        for slot in range(1, listing):
            listed = listed | (pos_ref[block * stride + 2 * panels + slot] == my_tile)

        @pl.when(listed & narrow)
        def _():
            per_block_narrow(block)

        @pl.when(listed & jnp.logical_not(narrow))
        def _():
            per_block_wide(block)

        return carry

    lax.fori_loop(0, blocks, per_block, 0)


def contact_sums(geometry, gathered, rows_x, cols_x):
    blocks = gathered.shape[0]
    smem = pl.BlockSpec(memory_space=pltpu.SMEM)
    vmem = pl.BlockSpec(memory_space=pltpu.VMEM)
    return pl.pallas_call(
        contact_kernel,
        out_shape=jax.ShapeDtypeStruct((blocks, 2, PAN_DEV, 128), jnp.float32),
        in_specs=[smem, smem, vmem, vmem],
        out_specs=vmem,
    )(geometry, gathered.reshape(-1), rows_x, cols_x)


def with_halo(block, sides, width):
    for axis, dim in sides:
        count = lax.axis_size(axis)
        forward = [(i, i + 1) for i in range(count - 1)]
        backward = [(target, source) for source, target in forward]
        narrow = dim == block.ndim - 1
        low = lax.slice_in_dim(block, block.shape[dim] - width, None, axis=dim)
        high = lax.slice_in_dim(block, 0, width, axis=dim)
        strip = low.shape
        if narrow:
            low, high = low.reshape(-1), high.reshape(-1)
        low = lax.ppermute(low, axis, forward).reshape(strip)
        high = lax.ppermute(high, axis, backward).reshape(strip)
        block = jnp.concatenate([low, block, high], axis=dim)
    return block


def bond_counts(bits, present_pad, rows, cols):
    kept_sum = jnp.zeros((rows, cols), jnp.float32)
    exist_sum = jnp.zeros((rows, cols), jnp.float32)
    for index, (row_off, col_off) in enumerate(offsets):
        present = present_pad[3 + row_off : 3 + row_off + rows, 3 + col_off : 3 + col_off + cols]
        flag = jnp.bitwise_and(jnp.right_shift(bits[index // 14], index % 14), 1).astype(
            jnp.float32
        )
        kept_sum = kept_sum + flag * present
        exist_sum = exist_sum + present
    return kept_sum, exist_sum


def forces(padded, bits, present_pad, rows, cols):
    centre = padded[:, 3 : 3 + rows, 3 : 3 + cols]
    total_row = jnp.zeros((rows, cols), jnp.float32)
    total_col = jnp.zeros((rows, cols), jnp.float32)
    kept_sum = jnp.zeros((rows, cols), jnp.float32)
    exist_sum = jnp.zeros((rows, cols), jnp.float32)
    for index, (row_off, col_off) in enumerate(offsets):
        other = padded[:, 3 + row_off : 3 + row_off + rows, 3 + col_off : 3 + col_off + cols]
        present = present_pad[3 + row_off : 3 + row_off + rows, 3 + col_off : 3 + col_off + cols]
        flag = jnp.bitwise_and(jnp.right_shift(bits[index // 14], index % 14), 1).astype(
            jnp.float32
        )
        keep = flag * present
        row_part = row_off + (other[0] - centre[0])
        col_part = col_off + (other[1] - centre[1])
        inv_length = lax.rsqrt(row_part * row_part + col_part * col_part)
        inv_rest = 1.0 / float((row_off * row_off + col_off * col_off) ** 0.5)
        coeff = keep * (inv_rest - inv_length)
        total_row = total_row + coeff * row_part
        total_col = total_col + coeff * col_part
        kept_sum = kept_sum + keep
        exist_sum = exist_sum + present
    return (jnp.stack([total_row, total_col]), kept_sum, exist_sum)


def body(disp, velocity, bond_bits, panel_pos, contact_list):
    rows, cols = (disp.shape[1], disp.shape[2])
    along_count = lax.axis_size("along")
    across_count = lax.axis_size("across")
    total_rows = rows * along_count
    total_cols = cols * across_count
    row_base = lax.axis_index("along") * rows
    col_base = lax.axis_index("across") * cols
    stacked = jnp.concatenate([disp, velocity, bond_bits.astype(jnp.float32)], axis=0)
    ext = with_halo(stacked, (("along", 1), ("across", 2)), 6)
    grid_row = row_base - 6 + jnp.arange(rows + 12, dtype=jnp.int32)
    grid_col = col_base - 6 + jnp.arange(cols + 12, dtype=jnp.int32)
    inside_row = (grid_row >= 0) & (grid_row < total_rows)
    inside_col = (grid_col >= 0) & (grid_col < total_cols)
    present_wide = (inside_row[:, None] & inside_col[None, :]).astype(jnp.float32)
    present_ring = present_wide[3:-3, 3:-3]
    force, _, _ = forces(
        ext[0:2], ext[4:6, 3:-3, 3:-3].astype(jnp.int32), present_wide, rows + 6, cols + 6
    )
    kept_sum, exist_sum = bond_counts(bond_bits, present_ring, rows, cols)
    damage = 1.0 - kept_sum / exist_sum
    ring_v = ext[2:4, 3:-3, 3:-3] + 10.0 * force
    ring_u = ext[0:2, 3:-3, 3:-3] + 0.05 * ring_v
    ring_u = jnp.where(present_ring[None] > 0.0, ring_u, 0.0)
    force, _, _ = forces(ring_u, bond_bits, present_ring, rows, cols)
    state_v = ring_v[:, 3:-3, 3:-3] + 10.0 * force
    state_u = ring_u[:, 3:-3, 3:-3] + 0.05 * state_v
    block_count = lax.axis_size("along")
    packed = jnp.concatenate(
        [panel_pos.reshape(1, -1), contact_list.astype(jnp.float32).reshape(1, -1)], axis=1
    )
    gathered = lax.all_to_all(
        jnp.broadcast_to(packed[None], (block_count,) + packed.shape), "along", 0, 0, tiled=True
    ).reshape(block_count, -1)
    gathered, state_u = lax.optimization_barrier((gathered, state_u))
    my_tile = lax.axis_index("along") * across_count + lax.axis_index("across")
    rows_x = (row_base + jnp.arange(rows, dtype=jnp.int32)).astype(jnp.float32)[:, None] + state_u[0]
    cols_x = (col_base + jnp.arange(cols, dtype=jnp.int32)).astype(jnp.float32)[None, :] + state_u[1]
    reach_row = 2.5 + jnp.max(jnp.abs(state_u[0]))
    reach_col = 2.5 + jnp.max(jnp.abs(state_u[1]))
    geometry = jnp.stack(
        [
            reach_row,
            reach_col,
            row_base.astype(jnp.float32),
            col_base.astype(jnp.float32),
            my_tile.astype(jnp.float32),
        ]
    )
    sums = contact_sums(geometry, gathered, rows_x, cols_x)
    partials = jnp.transpose(jnp.sum(sums, axis=-1), (0, 2, 1))
    spread = jnp.broadcast_to(
        partials.reshape(block_count, 1, 1, 2 * PAN_DEV),
        (block_count, across_count, 1, 2 * PAN_DEV),
    ).reshape(block_count * across_count, 1, 2 * PAN_DEV)
    arrived = lax.all_to_all(spread, ("along", "across"), 0, 0, tiled=True)
    panel_force = jnp.sum(arrived, axis=0).reshape(PAN_DEV, 2)
    return (state_u, state_v, damage, panel_force)


def solution(mesh):
    return jax.shard_map(
        body,
        mesh=mesh,
        in_specs=(
            P(None, "along", "across"),
            P(None, "along", "across"),
            P(None, "along", "across"),
            P("along", None),
            P("along", None),
        ),
        out_specs=(
            P(None, "along", "across"),
            P(None, "along", "across"),
            P("along", "across"),
            P("along", None),
        ),
        check_vma=False,
    )
```

```python
import jax
import jax.numpy as jnp
from jax import lax
from jax.experimental import pallas as pl
from jax.experimental.pallas import tpu as pltpu
from jax.sharding import PartitionSpec as P

PAN_DEV = 64


offsets = [(rr, cc) for rr in range(-3, 4) for cc in range(-3, 4) if 0 < rr * rr + cc * cc <= 9]


def contact_kernel(geo_ref, pos_ref, xr_ref, xc_ref, out_ref):
    out_ref[...] = jnp.zeros_like(out_ref)
    blocks = out_ref.shape[0]
    panels = PAN_DEV
    rows, cols = xr_ref.shape
    row_tiles = rows // 8
    col_tiles = cols // 128
    reach_row, reach_col = geo_ref[0], geo_ref[1]
    row_base, col_base, my_tile = geo_ref[2], geo_ref[3], geo_ref[4]
    stride = pos_ref.shape[0] // blocks
    listing = stride - 2 * panels
    empty = jnp.zeros((1, 128), jnp.float32)

    def window(centre, base, reach, size, group):
        local = centre - base
        low = jnp.clip((local - reach).astype(jnp.int32), 0, size)
        high = jnp.clip((local + reach).astype(jnp.int32) + 1, 0, size)
        first = low // group
        return first, jnp.maximum((high + group - 1) // group - first, 0)

    def tile_sums(centre_row, centre_col, row_group, col_group, accs):
        row = pl.multiple_of(row_group * 8, 8)
        col = pl.multiple_of(col_group * 128, 128)
        delta_row = centre_row - xr_ref[pl.ds(row, 8), pl.ds(col, 128)]
        delta_col = centre_col - xc_ref[pl.ds(row, 8), pl.ds(col, 128)]
        push = 0.5 * jnp.maximum(4.0 - delta_row * delta_row - delta_col * delta_col, 0.0)
        return (accs[0] + push * delta_row, accs[1] + push * delta_col)

    lane = lax.broadcasted_iota(jnp.int32, (1, 128), 1)

    def place(j, accs, sums):
        return (
            jnp.where(lane == j, jnp.sum(accs[0]), sums[0]),
            jnp.where(lane == j, jnp.sum(accs[1]), sums[1]),
        )

    def store(block, sums):
        out_ref[block, pl.ds(0, 1), :] = sums[0]
        out_ref[block, pl.ds(1, 1), :] = sums[1]

    zero = jnp.zeros((8, 128), jnp.float32)

    def per_block_narrow(block):
        def per_panel(j, sums):
            centre_row = pos_ref[block * stride + 2 * j]
            centre_col = pos_ref[block * stride + 2 * j + 1]
            first_row, _ = window(centre_row, row_base, reach_row, rows, 8)
            first_col, _ = window(centre_col, col_base, reach_col, cols, 128)
            first_row = jnp.minimum(first_row, row_tiles - 2)
            first_col = jnp.minimum(first_col, col_tiles - 2)
            accs = (zero, zero)
            for r in range(2):
                for c in range(2):
                    accs = tile_sums(centre_row, centre_col, first_row + r, first_col + c, accs)
            return place(j, accs, sums)

        store(block, lax.fori_loop(0, panels, per_panel, (empty, empty), unroll=8))

    def per_block_wide(block):
        def per_panel(j, sums):
            centre_row = pos_ref[block * stride + 2 * j]
            centre_col = pos_ref[block * stride + 2 * j + 1]
            first_row, row_groups = window(centre_row, row_base, reach_row, rows, 8)
            first_col, col_groups = window(centre_col, col_base, reach_col, cols, 128)

            def per_row(r, accs):
                def per_col(c, accs):
                    return tile_sums(centre_row, centre_col, first_row + r, first_col + c, accs)

                return lax.fori_loop(0, col_groups, per_col, accs)

            return place(j, lax.fori_loop(0, row_groups, per_row, (zero, zero)), sums)

        store(block, lax.fori_loop(0, panels, per_panel, (empty, empty)))

    narrow = (reach_row < 4.0) & (reach_col < 4.0)

    def per_block(block, carry):
        listed = pos_ref[block * stride + 2 * panels] == my_tile
        for slot in range(1, listing):
            listed = listed | (pos_ref[block * stride + 2 * panels + slot] == my_tile)

        @pl.when(listed & narrow)
        def _():
            per_block_narrow(block)

        @pl.when(listed & jnp.logical_not(narrow))
        def _():
            per_block_wide(block)

        return carry

    lax.fori_loop(0, blocks, per_block, 0)


def contact_sums(geometry, gathered, rows_x, cols_x):
    blocks = gathered.shape[0]
    smem = pl.BlockSpec(memory_space=pltpu.SMEM)
    vmem = pl.BlockSpec(memory_space=pltpu.VMEM)
    return pl.pallas_call(
        contact_kernel,
        out_shape=jax.ShapeDtypeStruct((blocks, 2, 128), jnp.float32),
        in_specs=[smem, smem, vmem, vmem],
        out_specs=vmem,
    )(geometry, gathered.reshape(-1), rows_x, cols_x)


def with_halo(block, sides, width):
    for axis, dim in sides:
        count = lax.axis_size(axis)
        forward = [(i, i + 1) for i in range(count - 1)]
        backward = [(target, source) for source, target in forward]
        narrow = dim == block.ndim - 1
        low = lax.slice_in_dim(block, block.shape[dim] - width, None, axis=dim)
        high = lax.slice_in_dim(block, 0, width, axis=dim)
        strip = low.shape
        if narrow:
            low, high = low.reshape(-1), high.reshape(-1)
        low = lax.ppermute(low, axis, forward).reshape(strip)
        high = lax.ppermute(high, axis, backward).reshape(strip)
        block = jnp.concatenate([low, block, high], axis=dim)
    return block


def bond_counts(bits, present_pad, rows, cols):
    kept_sum = jnp.zeros((rows, cols), jnp.float32)
    exist_sum = jnp.zeros((rows, cols), jnp.float32)
    for index, (row_off, col_off) in enumerate(offsets):
        present = present_pad[3 + row_off : 3 + row_off + rows, 3 + col_off : 3 + col_off + cols]
        flag = jnp.bitwise_and(jnp.right_shift(bits[index // 14], index % 14), 1).astype(
            jnp.float32
        )
        kept_sum = kept_sum + flag * present
        exist_sum = exist_sum + present
    return kept_sum, exist_sum


def forces(padded, bits, present_pad, rows, cols):
    centre = padded[:, 3 : 3 + rows, 3 : 3 + cols]
    total_row = jnp.zeros((rows, cols), jnp.float32)
    total_col = jnp.zeros((rows, cols), jnp.float32)
    kept_sum = jnp.zeros((rows, cols), jnp.float32)
    exist_sum = jnp.zeros((rows, cols), jnp.float32)
    for index, (row_off, col_off) in enumerate(offsets):
        other = padded[:, 3 + row_off : 3 + row_off + rows, 3 + col_off : 3 + col_off + cols]
        present = present_pad[3 + row_off : 3 + row_off + rows, 3 + col_off : 3 + col_off + cols]
        flag = jnp.bitwise_and(jnp.right_shift(bits[index // 14], index % 14), 1).astype(
            jnp.float32
        )
        keep = flag * present
        row_part = row_off + (other[0] - centre[0])
        col_part = col_off + (other[1] - centre[1])
        inv_length = lax.rsqrt(row_part * row_part + col_part * col_part)
        inv_rest = 1.0 / float((row_off * row_off + col_off * col_off) ** 0.5)
        coeff = keep * (inv_rest - inv_length)
        total_row = total_row + coeff * row_part
        total_col = total_col + coeff * col_part
        kept_sum = kept_sum + keep
        exist_sum = exist_sum + present
    return (jnp.stack([total_row, total_col]), kept_sum, exist_sum)


def body(disp, velocity, bond_bits, panel_pos, contact_list):
    rows, cols = (disp.shape[1], disp.shape[2])
    along_count = lax.axis_size("along")
    across_count = lax.axis_size("across")
    total_rows = rows * along_count
    total_cols = cols * across_count
    row_base = lax.axis_index("along") * rows
    col_base = lax.axis_index("across") * cols
    stacked = jnp.concatenate([disp, velocity, bond_bits.astype(jnp.float32)], axis=0)
    ext = with_halo(stacked, (("along", 1), ("across", 2)), 6)
    grid_row = row_base - 6 + jnp.arange(rows + 12, dtype=jnp.int32)
    grid_col = col_base - 6 + jnp.arange(cols + 12, dtype=jnp.int32)
    inside_row = (grid_row >= 0) & (grid_row < total_rows)
    inside_col = (grid_col >= 0) & (grid_col < total_cols)
    present_wide = (inside_row[:, None] & inside_col[None, :]).astype(jnp.float32)
    present_ring = present_wide[3:-3, 3:-3]
    force, _, _ = forces(
        ext[0:2], ext[4:6, 3:-3, 3:-3].astype(jnp.int32), present_wide, rows + 6, cols + 6
    )
    kept_sum, exist_sum = bond_counts(bond_bits, present_ring, rows, cols)
    damage = 1.0 - kept_sum / exist_sum
    ring_v = ext[2:4, 3:-3, 3:-3] + 10.0 * force
    ring_u = ext[0:2, 3:-3, 3:-3] + 0.05 * ring_v
    ring_u = jnp.where(present_ring[None] > 0.0, ring_u, 0.0)
    force, _, _ = forces(ring_u, bond_bits, present_ring, rows, cols)
    state_v = ring_v[:, 3:-3, 3:-3] + 10.0 * force
    state_u = ring_u[:, 3:-3, 3:-3] + 0.05 * state_v
    block_count = lax.axis_size("along")
    packed = jnp.concatenate(
        [panel_pos.reshape(1, -1), contact_list.astype(jnp.float32).reshape(1, -1)], axis=1
    )
    gathered = lax.all_to_all(
        jnp.broadcast_to(packed[None], (block_count,) + packed.shape), "along", 0, 0, tiled=True
    ).reshape(block_count, -1)
    gathered, state_u = lax.optimization_barrier((gathered, state_u))
    my_tile = lax.axis_index("along") * across_count + lax.axis_index("across")
    rows_x = (row_base + jnp.arange(rows, dtype=jnp.int32)).astype(jnp.float32)[:, None] + state_u[0]
    cols_x = (col_base + jnp.arange(cols, dtype=jnp.int32)).astype(jnp.float32)[None, :] + state_u[1]
    reach_row = 2.5 + jnp.max(jnp.abs(state_u[0]))
    reach_col = 2.5 + jnp.max(jnp.abs(state_u[1]))
    geometry = jnp.stack(
        [
            reach_row,
            reach_col,
            row_base.astype(jnp.float32),
            col_base.astype(jnp.float32),
            my_tile.astype(jnp.float32),
        ]
    )
    sums = contact_sums(geometry, gathered, rows_x, cols_x)
    partials = jnp.transpose(sums[:, :, :PAN_DEV], (0, 2, 1))
    spread = jnp.broadcast_to(
        partials.reshape(block_count, 1, 1, 2 * PAN_DEV),
        (block_count, across_count, 1, 2 * PAN_DEV),
    ).reshape(block_count * across_count, 1, 2 * PAN_DEV)
    arrived = lax.all_to_all(spread, ("along", "across"), 0, 0, tiled=True)
    panel_force = jnp.sum(arrived, axis=0).reshape(PAN_DEV, 2)
    return (state_u, state_v, damage, panel_force)


def solution(mesh):
    return jax.shard_map(
        body,
        mesh=mesh,
        in_specs=(
            P(None, "along", "across"),
            P(None, "along", "across"),
            P(None, "along", "across"),
            P("along", None),
            P("along", None),
        ),
        out_specs=(
            P(None, "along", "across"),
            P(None, "along", "across"),
            P("along", "across"),
            P("along", None),
        ),
        check_vma=False,
    )
```

```python
import jax
import jax.numpy as jnp
from jax import lax
from jax.experimental import pallas as pl
from jax.experimental.pallas import tpu as pltpu
from jax.sharding import PartitionSpec as P

PAN_DEV = 64


offsets = [(rr, cc) for rr in range(-3, 4) for cc in range(-3, 4) if 0 < rr * rr + cc * cc <= 9]


def contact_kernel(geo_ref, pos_ref, xr_ref, xc_ref, out_ref):
    out_ref[...] = jnp.zeros_like(out_ref)
    blocks, _, panels, _ = out_ref.shape
    rows, cols = xr_ref.shape
    row_tiles = rows // 8
    col_tiles = cols // 128
    reach_row, reach_col = geo_ref[0], geo_ref[1]
    row_base, col_base, my_tile = geo_ref[2], geo_ref[3], geo_ref[4]
    stride = pos_ref.shape[0] // blocks
    listing = stride - 2 * panels

    def window(centre, base, reach, size, group):
        local = centre - base
        low = jnp.clip((local - reach).astype(jnp.int32), 0, size)
        high = jnp.clip((local + reach).astype(jnp.int32) + 1, 0, size)
        first = low // group
        return first, jnp.maximum((high + group - 1) // group - first, 0)

    def tile_sums(centre_row, centre_col, row_group, col_group, accs):
        row = pl.multiple_of(row_group * 8, 8)
        col = pl.multiple_of(col_group * 128, 128)
        delta_row = centre_row - xr_ref[pl.ds(row, 8), pl.ds(col, 128)]
        delta_col = centre_col - xc_ref[pl.ds(row, 8), pl.ds(col, 128)]
        push = 0.5 * jnp.maximum(4.0 - delta_row * delta_row - delta_col * delta_col, 0.0)
        return (accs[0] + push * delta_row, accs[1] + push * delta_col)

    def store(block, j, accs):
        out_ref[block, 0, pl.ds(j, 1), :] = jnp.sum(accs[0], axis=0, keepdims=True)
        out_ref[block, 1, pl.ds(j, 1), :] = jnp.sum(accs[1], axis=0, keepdims=True)

    zero = jnp.zeros((8, 128), jnp.float32)

    def per_block_narrow(block):
        def per_panel(j, carry):
            centre_row = pos_ref[block * stride + 2 * j]
            centre_col = pos_ref[block * stride + 2 * j + 1]
            first_row, _ = window(centre_row, row_base, reach_row, rows, 8)
            first_col, _ = window(centre_col, col_base, reach_col, cols, 128)
            first_row = jnp.minimum(first_row, row_tiles - 2)
            first_col = jnp.minimum(first_col, col_tiles - 2)
            accs = (zero, zero)
            for r in range(2):
                for c in range(2):
                    accs = tile_sums(centre_row, centre_col, first_row + r, first_col + c, accs)
            store(block, j, accs)
            return carry

        lax.fori_loop(0, panels, per_panel, 0, unroll=8)

    def per_block_wide(block):
        def per_panel(j, carry):
            centre_row = pos_ref[block * stride + 2 * j]
            centre_col = pos_ref[block * stride + 2 * j + 1]
            first_row, row_groups = window(centre_row, row_base, reach_row, rows, 8)
            first_col, col_groups = window(centre_col, col_base, reach_col, cols, 128)

            def per_row(r, accs):
                def per_col(c, accs):
                    return tile_sums(centre_row, centre_col, first_row + r, first_col + c, accs)

                return lax.fori_loop(0, col_groups, per_col, accs)

            store(block, j, lax.fori_loop(0, row_groups, per_row, (zero, zero)))
            return carry

        lax.fori_loop(0, panels, per_panel, 0)

    narrow = (reach_row < 4.0) & (reach_col < 4.0)

    def per_block(block, carry):
        listed = pos_ref[block * stride + 2 * panels] == my_tile
        for slot in range(1, listing):
            listed = listed | (pos_ref[block * stride + 2 * panels + slot] == my_tile)

        @pl.when(listed & narrow)
        def _():
            per_block_narrow(block)

        @pl.when(listed & jnp.logical_not(narrow))
        def _():
            per_block_wide(block)

        return carry

    lax.fori_loop(0, blocks, per_block, 0)


def contact_sums(geometry, gathered, rows_x, cols_x):
    blocks = gathered.shape[0]
    smem = pl.BlockSpec(memory_space=pltpu.SMEM)
    vmem = pl.BlockSpec(memory_space=pltpu.VMEM)
    return pl.pallas_call(
        contact_kernel,
        out_shape=jax.ShapeDtypeStruct((blocks, 2, PAN_DEV, 128), jnp.float32),
        in_specs=[smem, smem, vmem, vmem],
        out_specs=vmem,
    )(geometry, gathered.reshape(-1), rows_x, cols_x)


def with_halo(block, sides, width):
    for axis, dim in sides:
        count = lax.axis_size(axis)
        forward = [(i, i + 1) for i in range(count - 1)]
        backward = [(target, source) for source, target in forward]
        narrow = dim == block.ndim - 1
        low = lax.slice_in_dim(block, block.shape[dim] - width, None, axis=dim)
        high = lax.slice_in_dim(block, 0, width, axis=dim)
        strip = low.shape
        if narrow:
            low, high = low.reshape(-1), high.reshape(-1)
        low = lax.ppermute(low, axis, forward).reshape(strip)
        high = lax.ppermute(high, axis, backward).reshape(strip)
        block = jnp.concatenate([low, block, high], axis=dim)
    return block


def bond_counts(bits, present_pad, rows, cols):
    kept_sum = jnp.zeros((rows, cols), jnp.float32)
    exist_sum = jnp.zeros((rows, cols), jnp.float32)
    for index, (row_off, col_off) in enumerate(offsets):
        present = present_pad[3 + row_off : 3 + row_off + rows, 3 + col_off : 3 + col_off + cols]
        flag = jnp.bitwise_and(jnp.right_shift(bits[index // 14], index % 14), 1).astype(
            jnp.float32
        )
        kept_sum = kept_sum + flag * present
        exist_sum = exist_sum + present
    return kept_sum, exist_sum


def forces(padded, bits, rows, cols):
    centre = padded[:, 3 : 3 + rows, 3 : 3 + cols]
    total_row = jnp.zeros((rows, cols), jnp.float32)
    total_col = jnp.zeros((rows, cols), jnp.float32)
    for index, (row_off, col_off) in enumerate(offsets):
        other = padded[:, 3 + row_off : 3 + row_off + rows, 3 + col_off : 3 + col_off + cols]
        keep = jnp.bitwise_and(jnp.right_shift(bits[index // 14], index % 14), 1).astype(
            jnp.float32
        )
        row_part = row_off + (other[0] - centre[0])
        col_part = col_off + (other[1] - centre[1])
        inv_length = lax.rsqrt(row_part * row_part + col_part * col_part)
        inv_rest = 1.0 / float((row_off * row_off + col_off * col_off) ** 0.5)
        coeff = keep * (inv_rest - inv_length)
        total_row = total_row + coeff * row_part
        total_col = total_col + coeff * col_part
    return jnp.stack([total_row, total_col])


def body(disp, velocity, bond_bits, panel_pos, contact_list):
    rows, cols = (disp.shape[1], disp.shape[2])
    along_count = lax.axis_size("along")
    across_count = lax.axis_size("across")
    total_rows = rows * along_count
    total_cols = cols * across_count
    row_base = lax.axis_index("along") * rows
    col_base = lax.axis_index("across") * cols
    stacked = jnp.concatenate([disp, velocity, bond_bits.astype(jnp.float32)], axis=0)
    ext = with_halo(stacked, (("along", 1), ("across", 2)), 6)
    grid_row = row_base - 6 + jnp.arange(rows + 12, dtype=jnp.int32)
    grid_col = col_base - 6 + jnp.arange(cols + 12, dtype=jnp.int32)
    inside_row = (grid_row >= 0) & (grid_row < total_rows)
    inside_col = (grid_col >= 0) & (grid_col < total_cols)
    present_wide = (inside_row[:, None] & inside_col[None, :]).astype(jnp.float32)
    present_ring = present_wide[3:-3, 3:-3]
    ring_bits = ext[4:6, 3:-3, 3:-3].astype(jnp.int32)
    words = [jnp.zeros((rows + 6, cols + 6), jnp.int32) for _ in range(2)]
    for index, (row_off, col_off) in enumerate(offsets):
        inside = present_wide[3 + row_off : 3 + row_off + rows + 6, 3 + col_off : 3 + col_off + cols + 6]
        words[index // 14] = words[index // 14] | jnp.left_shift(
            inside.astype(jnp.int32), index % 14
        )
    ring_bits = jnp.bitwise_and(ring_bits, jnp.stack(words))
    force = forces(ext[0:2], ring_bits, rows + 6, cols + 6)
    kept_sum, exist_sum = bond_counts(bond_bits, present_ring, rows, cols)
    damage = 1.0 - kept_sum / exist_sum
    ring_v = ext[2:4, 3:-3, 3:-3] + 10.0 * force
    ring_u = ext[0:2, 3:-3, 3:-3] + 0.05 * ring_v
    ring_u = jnp.where(present_ring[None] > 0.0, ring_u, 0.0)
    force = forces(ring_u, ring_bits[:, 3:-3, 3:-3], rows, cols)
    state_v = ring_v[:, 3:-3, 3:-3] + 10.0 * force
    state_u = ring_u[:, 3:-3, 3:-3] + 0.05 * state_v
    block_count = lax.axis_size("along")
    packed = jnp.concatenate(
        [panel_pos.reshape(1, -1), contact_list.astype(jnp.float32).reshape(1, -1)], axis=1
    )
    gathered = lax.all_to_all(
        jnp.broadcast_to(packed[None], (block_count,) + packed.shape), "along", 0, 0, tiled=True
    ).reshape(block_count, -1)
    gathered, state_u = lax.optimization_barrier((gathered, state_u))
    my_tile = lax.axis_index("along") * across_count + lax.axis_index("across")
    rows_x = (row_base + jnp.arange(rows, dtype=jnp.int32)).astype(jnp.float32)[:, None] + state_u[0]
    cols_x = (col_base + jnp.arange(cols, dtype=jnp.int32)).astype(jnp.float32)[None, :] + state_u[1]
    reach_row = 2.5 + jnp.max(jnp.abs(state_u[0]))
    reach_col = 2.5 + jnp.max(jnp.abs(state_u[1]))
    geometry = jnp.stack(
        [
            reach_row,
            reach_col,
            row_base.astype(jnp.float32),
            col_base.astype(jnp.float32),
            my_tile.astype(jnp.float32),
        ]
    )
    sums = contact_sums(geometry, gathered, rows_x, cols_x)
    partials = jnp.transpose(jnp.sum(sums, axis=-1), (0, 2, 1))
    spread = jnp.broadcast_to(
        partials.reshape(block_count, 1, 1, 2 * PAN_DEV),
        (block_count, across_count, 1, 2 * PAN_DEV),
    ).reshape(block_count * across_count, 1, 2 * PAN_DEV)
    arrived = lax.all_to_all(spread, ("along", "across"), 0, 0, tiled=True)
    panel_force = jnp.sum(arrived, axis=0).reshape(PAN_DEV, 2)
    return (state_u, state_v, damage, panel_force)


def solution(mesh):
    return jax.shard_map(
        body,
        mesh=mesh,
        in_specs=(
            P(None, "along", "across"),
            P(None, "along", "across"),
            P(None, "along", "across"),
            P("along", None),
            P("along", None),
        ),
        out_specs=(
            P(None, "along", "across"),
            P(None, "along", "across"),
            P("along", "across"),
            P("along", None),
        ),
        check_vma=False,
    )
```

```python
import jax
import jax.numpy as jnp
from jax import lax
from jax.experimental import pallas as pl
from jax.experimental.pallas import tpu as pltpu
from jax.sharding import PartitionSpec as P

PAN_DEV = 64


offsets = [(rr, cc) for rr in range(-3, 4) for cc in range(-3, 4) if 0 < rr * rr + cc * cc <= 9]


def contact_kernel(geo_ref, pos_ref, xr_ref, xc_ref, out_ref):
    out_ref[...] = jnp.zeros_like(out_ref)
    blocks, _, panels, _ = out_ref.shape
    rows, cols = xr_ref.shape
    row_tiles = rows // 8
    col_tiles = cols // 128
    reach_row, reach_col = geo_ref[0], geo_ref[1]
    row_base, col_base, my_tile = geo_ref[2], geo_ref[3], geo_ref[4]
    stride = pos_ref.shape[0] // blocks
    listing = stride - 2 * panels

    def window(centre, base, reach, size, group):
        local = centre - base
        low = jnp.clip((local - reach).astype(jnp.int32), 0, size)
        high = jnp.clip((local + reach).astype(jnp.int32) + 1, 0, size)
        first = low // group
        return first, jnp.maximum((high + group - 1) // group - first, 0)

    def tile_sums(centre_row, centre_col, row_group, col_group, accs):
        row = pl.multiple_of(row_group * 8, 8)
        col = pl.multiple_of(col_group * 128, 128)
        delta_row = centre_row - xr_ref[pl.ds(row, 8), pl.ds(col, 128)]
        delta_col = centre_col - xc_ref[pl.ds(row, 8), pl.ds(col, 128)]
        push = 0.5 * jnp.maximum(4.0 - delta_row * delta_row - delta_col * delta_col, 0.0)
        return (accs[0] + push * delta_row, accs[1] + push * delta_col)

    def store(block, j, accs):
        out_ref[block, 0, pl.ds(j, 1), :] = jnp.sum(accs[0], axis=0, keepdims=True)
        out_ref[block, 1, pl.ds(j, 1), :] = jnp.sum(accs[1], axis=0, keepdims=True)

    zero = jnp.zeros((8, 128), jnp.float32)

    def per_block_narrow(block):
        def per_panel(j, carry):
            centre_row = pos_ref[block * stride + 2 * j]
            centre_col = pos_ref[block * stride + 2 * j + 1]
            first_row, _ = window(centre_row, row_base, reach_row, rows, 8)
            first_col, _ = window(centre_col, col_base, reach_col, cols, 128)
            first_row = jnp.minimum(first_row, row_tiles - 2)
            first_col = jnp.minimum(first_col, col_tiles - 2)
            accs = (zero, zero)
            for r in range(2):
                for c in range(2):
                    accs = tile_sums(centre_row, centre_col, first_row + r, first_col + c, accs)
            store(block, j, accs)
            return carry

        lax.fori_loop(0, panels, per_panel, 0, unroll=8)

    def per_block_wide(block):
        def per_panel(j, carry):
            centre_row = pos_ref[block * stride + 2 * j]
            centre_col = pos_ref[block * stride + 2 * j + 1]
            first_row, row_groups = window(centre_row, row_base, reach_row, rows, 8)
            first_col, col_groups = window(centre_col, col_base, reach_col, cols, 128)

            def per_row(r, accs):
                def per_col(c, accs):
                    return tile_sums(centre_row, centre_col, first_row + r, first_col + c, accs)

                return lax.fori_loop(0, col_groups, per_col, accs)

            store(block, j, lax.fori_loop(0, row_groups, per_row, (zero, zero)))
            return carry

        lax.fori_loop(0, panels, per_panel, 0)

    narrow = (reach_row < 4.0) & (reach_col < 4.0)

    def per_block(block, carry):
        listed = pos_ref[block * stride + 2 * panels] == my_tile
        for slot in range(1, listing):
            listed = listed | (pos_ref[block * stride + 2 * panels + slot] == my_tile)

        @pl.when(listed & narrow)
        def _():
            per_block_narrow(block)

        @pl.when(listed & jnp.logical_not(narrow))
        def _():
            per_block_wide(block)

        return carry

    lax.fori_loop(0, blocks, per_block, 0)


def contact_sums(geometry, gathered, rows_x, cols_x):
    blocks = gathered.shape[0]
    smem = pl.BlockSpec(memory_space=pltpu.SMEM)
    vmem = pl.BlockSpec(memory_space=pltpu.VMEM)
    return pl.pallas_call(
        contact_kernel,
        out_shape=jax.ShapeDtypeStruct((blocks, 2, PAN_DEV, 128), jnp.float32),
        in_specs=[smem, smem, vmem, vmem],
        out_specs=vmem,
    )(geometry, gathered.reshape(-1), rows_x, cols_x)


def with_halo(block, sides, width):
    for axis, dim in sides:
        count = lax.axis_size(axis)
        forward = [(i, i + 1) for i in range(count - 1)]
        backward = [(target, source) for source, target in forward]
        narrow = dim == block.ndim - 1
        low = lax.slice_in_dim(block, block.shape[dim] - width, None, axis=dim)
        high = lax.slice_in_dim(block, 0, width, axis=dim)
        strip = low.shape
        if narrow:
            low, high = low.reshape(-1), high.reshape(-1)
        low = lax.ppermute(low, axis, forward).reshape(strip)
        high = lax.ppermute(high, axis, backward).reshape(strip)
        block = jnp.concatenate([low, block, high], axis=dim)
    return block


def bond_counts(bits, present_pad, rows, cols):
    kept_sum = jnp.zeros((rows, cols), jnp.float32)
    exist_sum = jnp.zeros((rows, cols), jnp.float32)
    for index, (row_off, col_off) in enumerate(offsets):
        present = present_pad[3 + row_off : 3 + row_off + rows, 3 + col_off : 3 + col_off + cols]
        flag = jnp.bitwise_and(jnp.right_shift(bits[index // 14], index % 14), 1).astype(
            jnp.float32
        )
        kept_sum = kept_sum + flag * present
        exist_sum = exist_sum + present
    return kept_sum, exist_sum


def forces(padded, bits, rows, cols):
    centre = padded[:, 3 : 3 + rows, 3 : 3 + cols]
    total_row = jnp.zeros((rows, cols), jnp.float32)
    total_col = jnp.zeros((rows, cols), jnp.float32)
    for index, (row_off, col_off) in enumerate(offsets):
        other = padded[:, 3 + row_off : 3 + row_off + rows, 3 + col_off : 3 + col_off + cols]
        keep = jnp.bitwise_and(jnp.right_shift(bits[index // 14], index % 14), 1).astype(
            jnp.float32
        )
        row_part = row_off + (other[0] - centre[0])
        col_part = col_off + (other[1] - centre[1])
        inv_length = lax.rsqrt(row_part * row_part + col_part * col_part)
        inv_rest = 1.0 / float((row_off * row_off + col_off * col_off) ** 0.5)
        coeff = keep * (inv_rest - inv_length)
        total_row = total_row + coeff * row_part
        total_col = total_col + coeff * col_part
    return jnp.stack([total_row, total_col])


def body(disp, velocity, bond_bits, panel_pos, contact_list):
    rows, cols = (disp.shape[1], disp.shape[2])
    along_count = lax.axis_size("along")
    across_count = lax.axis_size("across")
    total_rows = rows * along_count
    total_cols = cols * across_count
    row_base = lax.axis_index("along") * rows
    col_base = lax.axis_index("across") * cols
    stacked = jnp.concatenate([disp, velocity, bond_bits.astype(jnp.float32)], axis=0)
    ext = with_halo(stacked, (("along", 1), ("across", 2)), 6)
    grid_row = row_base - 6 + jnp.arange(rows + 12, dtype=jnp.int32)
    grid_col = col_base - 6 + jnp.arange(cols + 12, dtype=jnp.int32)
    inside_row = (grid_row >= 0) & (grid_row < total_rows)
    inside_col = (grid_col >= 0) & (grid_col < total_cols)
    present_wide = (inside_row[:, None] & inside_col[None, :]).astype(jnp.float32)
    present_ring = present_wide[3:-3, 3:-3]
    ring_bits = ext[4:6, 3:-3, 3:-3].astype(jnp.int32)
    row_words = [jnp.zeros((rows + 6,), jnp.int32) for _ in range(2)]
    col_words = [jnp.zeros((cols + 6,), jnp.int32) for _ in range(2)]
    for index, (row_off, col_off) in enumerate(offsets):
        word, bit = index // 14, index % 14
        row_in = inside_row[3 + row_off : 3 + row_off + rows + 6].astype(jnp.int32)
        col_in = inside_col[3 + col_off : 3 + col_off + cols + 6].astype(jnp.int32)
        row_words[word] = row_words[word] | jnp.left_shift(row_in, bit)
        col_words[word] = col_words[word] | jnp.left_shift(col_in, bit)
    words = jnp.stack([row_words[w][:, None] & col_words[w][None, :] for w in range(2)])
    ring_bits = jnp.bitwise_and(ring_bits, words)
    force = forces(ext[0:2], ring_bits, rows + 6, cols + 6)
    kept_sum, exist_sum = bond_counts(bond_bits, present_ring, rows, cols)
    damage = 1.0 - kept_sum / exist_sum
    ring_v = ext[2:4, 3:-3, 3:-3] + 10.0 * force
    ring_u = ext[0:2, 3:-3, 3:-3] + 0.05 * ring_v
    ring_u = jnp.where(present_ring[None] > 0.0, ring_u, 0.0)
    force = forces(ring_u, ring_bits[:, 3:-3, 3:-3], rows, cols)
    state_v = ring_v[:, 3:-3, 3:-3] + 10.0 * force
    state_u = ring_u[:, 3:-3, 3:-3] + 0.05 * state_v
    block_count = lax.axis_size("along")
    packed = jnp.concatenate(
        [panel_pos.reshape(1, -1), contact_list.astype(jnp.float32).reshape(1, -1)], axis=1
    )
    gathered = lax.all_to_all(
        jnp.broadcast_to(packed[None], (block_count,) + packed.shape), "along", 0, 0, tiled=True
    ).reshape(block_count, -1)
    gathered, state_u = lax.optimization_barrier((gathered, state_u))
    my_tile = lax.axis_index("along") * across_count + lax.axis_index("across")
    rows_x = (row_base + jnp.arange(rows, dtype=jnp.int32)).astype(jnp.float32)[:, None] + state_u[0]
    cols_x = (col_base + jnp.arange(cols, dtype=jnp.int32)).astype(jnp.float32)[None, :] + state_u[1]
    reach_row = 2.5 + jnp.max(jnp.abs(state_u[0]))
    reach_col = 2.5 + jnp.max(jnp.abs(state_u[1]))
    geometry = jnp.stack(
        [
            reach_row,
            reach_col,
            row_base.astype(jnp.float32),
            col_base.astype(jnp.float32),
            my_tile.astype(jnp.float32),
        ]
    )
    sums = contact_sums(geometry, gathered, rows_x, cols_x)
    partials = jnp.transpose(jnp.sum(sums, axis=-1), (0, 2, 1))
    spread = jnp.broadcast_to(
        partials.reshape(block_count, 1, 1, 2 * PAN_DEV),
        (block_count, across_count, 1, 2 * PAN_DEV),
    ).reshape(block_count * across_count, 1, 2 * PAN_DEV)
    arrived = lax.all_to_all(spread, ("along", "across"), 0, 0, tiled=True)
    panel_force = jnp.sum(arrived, axis=0).reshape(PAN_DEV, 2)
    return (state_u, state_v, damage, panel_force)


def solution(mesh):
    return jax.shard_map(
        body,
        mesh=mesh,
        in_specs=(
            P(None, "along", "across"),
            P(None, "along", "across"),
            P(None, "along", "across"),
            P("along", None),
            P("along", None),
        ),
        out_specs=(
            P(None, "along", "across"),
            P(None, "along", "across"),
            P("along", "across"),
            P("along", None),
        ),
        check_vma=False,
    )
```

```python
import jax
import jax.numpy as jnp
from jax import lax
from jax.experimental import pallas as pl
from jax.experimental.pallas import tpu as pltpu
from jax.sharding import PartitionSpec as P

PAN_DEV = 64


offsets = [(rr, cc) for rr in range(-3, 4) for cc in range(-3, 4) if 0 < rr * rr + cc * cc <= 9]


def contact_kernel(geo_ref, pos_ref, xr_ref, xc_ref, out_ref):
    blocks, _, panels, _ = out_ref.shape
    rows, cols = xr_ref.shape
    row_tiles = rows // 8
    col_tiles = cols // 128
    reach_row, reach_col = geo_ref[0], geo_ref[1]
    row_base, col_base, my_tile = geo_ref[2], geo_ref[3], geo_ref[4]
    stride = pos_ref.shape[0] // blocks
    listing = stride - 2 * panels

    def window(centre, base, reach, size, group):
        local = centre - base
        low = jnp.clip((local - reach).astype(jnp.int32), 0, size)
        high = jnp.clip((local + reach).astype(jnp.int32) + 1, 0, size)
        first = low // group
        return first, jnp.maximum((high + group - 1) // group - first, 0)

    def tile_sums(centre_row, centre_col, row_group, col_group, accs):
        row = pl.multiple_of(row_group * 8, 8)
        col = pl.multiple_of(col_group * 128, 128)
        delta_row = centre_row - xr_ref[pl.ds(row, 8), pl.ds(col, 128)]
        delta_col = centre_col - xc_ref[pl.ds(row, 8), pl.ds(col, 128)]
        push = 0.5 * jnp.maximum(4.0 - delta_row * delta_row - delta_col * delta_col, 0.0)
        return (accs[0] + push * delta_row, accs[1] + push * delta_col)

    def store(block, j, accs):
        out_ref[block, 0, pl.ds(j, 1), :] = jnp.sum(accs[0], axis=0, keepdims=True)
        out_ref[block, 1, pl.ds(j, 1), :] = jnp.sum(accs[1], axis=0, keepdims=True)

    zero = jnp.zeros((8, 128), jnp.float32)

    def per_block_narrow(block):
        def per_panel(j, carry):
            centre_row = pos_ref[block * stride + 2 * j]
            centre_col = pos_ref[block * stride + 2 * j + 1]
            first_row, _ = window(centre_row, row_base, reach_row, rows, 8)
            first_col, _ = window(centre_col, col_base, reach_col, cols, 128)
            first_row = jnp.minimum(first_row, row_tiles - 2)
            first_col = jnp.minimum(first_col, col_tiles - 2)
            accs = (zero, zero)
            for r in range(2):
                for c in range(2):
                    accs = tile_sums(centre_row, centre_col, first_row + r, first_col + c, accs)
            store(block, j, accs)
            return carry

        lax.fori_loop(0, panels, per_panel, 0, unroll=8)

    def per_block_wide(block):
        def per_panel(j, carry):
            centre_row = pos_ref[block * stride + 2 * j]
            centre_col = pos_ref[block * stride + 2 * j + 1]
            first_row, row_groups = window(centre_row, row_base, reach_row, rows, 8)
            first_col, col_groups = window(centre_col, col_base, reach_col, cols, 128)

            def per_row(r, accs):
                def per_col(c, accs):
                    return tile_sums(centre_row, centre_col, first_row + r, first_col + c, accs)

                return lax.fori_loop(0, col_groups, per_col, accs)

            store(block, j, lax.fori_loop(0, row_groups, per_row, (zero, zero)))
            return carry

        lax.fori_loop(0, panels, per_panel, 0)

    narrow = (reach_row < 4.0) & (reach_col < 4.0)

    def per_block(block, carry):
        listed = pos_ref[block * stride + 2 * panels] == my_tile
        for slot in range(1, listing):
            listed = listed | (pos_ref[block * stride + 2 * panels + slot] == my_tile)

        @pl.when(jnp.logical_not(listed))
        def _():
            out_ref[block] = jnp.zeros(out_ref.shape[1:], out_ref.dtype)

        @pl.when(listed & narrow)
        def _():
            per_block_narrow(block)

        @pl.when(listed & jnp.logical_not(narrow))
        def _():
            per_block_wide(block)

        return carry

    lax.fori_loop(0, blocks, per_block, 0)


def contact_sums(geometry, gathered, rows_x, cols_x):
    blocks = gathered.shape[0]
    smem = pl.BlockSpec(memory_space=pltpu.SMEM)
    vmem = pl.BlockSpec(memory_space=pltpu.VMEM)
    return pl.pallas_call(
        contact_kernel,
        out_shape=jax.ShapeDtypeStruct((blocks, 2, PAN_DEV, 128), jnp.float32),
        in_specs=[smem, smem, vmem, vmem],
        out_specs=vmem,
    )(geometry, gathered.reshape(-1), rows_x, cols_x)


def with_halo(block, sides, width):
    for axis, dim in sides:
        count = lax.axis_size(axis)
        forward = [(i, i + 1) for i in range(count - 1)]
        backward = [(target, source) for source, target in forward]
        narrow = dim == block.ndim - 1
        low = lax.slice_in_dim(block, block.shape[dim] - width, None, axis=dim)
        high = lax.slice_in_dim(block, 0, width, axis=dim)
        strip = low.shape
        if narrow:
            low, high = low.reshape(-1), high.reshape(-1)
        low = lax.ppermute(low, axis, forward).reshape(strip)
        high = lax.ppermute(high, axis, backward).reshape(strip)
        block = jnp.concatenate([low, block, high], axis=dim)
    return block


def bond_counts(bits, present_pad, rows, cols):
    kept_sum = jnp.zeros((rows, cols), jnp.float32)
    exist_sum = jnp.zeros((rows, cols), jnp.float32)
    for index, (row_off, col_off) in enumerate(offsets):
        present = present_pad[3 + row_off : 3 + row_off + rows, 3 + col_off : 3 + col_off + cols]
        flag = jnp.bitwise_and(jnp.right_shift(bits[index // 14], index % 14), 1).astype(
            jnp.float32
        )
        kept_sum = kept_sum + flag * present
        exist_sum = exist_sum + present
    return kept_sum, exist_sum


def forces(padded, bits, rows, cols):
    centre = padded[:, 3 : 3 + rows, 3 : 3 + cols]
    total_row = jnp.zeros((rows, cols), jnp.float32)
    total_col = jnp.zeros((rows, cols), jnp.float32)
    for index, (row_off, col_off) in enumerate(offsets):
        other = padded[:, 3 + row_off : 3 + row_off + rows, 3 + col_off : 3 + col_off + cols]
        keep = jnp.bitwise_and(jnp.right_shift(bits[index // 14], index % 14), 1).astype(
            jnp.float32
        )
        row_part = row_off + (other[0] - centre[0])
        col_part = col_off + (other[1] - centre[1])
        inv_length = lax.rsqrt(row_part * row_part + col_part * col_part)
        inv_rest = 1.0 / float((row_off * row_off + col_off * col_off) ** 0.5)
        coeff = keep * (inv_rest - inv_length)
        total_row = total_row + coeff * row_part
        total_col = total_col + coeff * col_part
    return jnp.stack([total_row, total_col])


def body(disp, velocity, bond_bits, panel_pos, contact_list):
    rows, cols = (disp.shape[1], disp.shape[2])
    along_count = lax.axis_size("along")
    across_count = lax.axis_size("across")
    total_rows = rows * along_count
    total_cols = cols * across_count
    row_base = lax.axis_index("along") * rows
    col_base = lax.axis_index("across") * cols
    stacked = jnp.concatenate([disp, velocity, bond_bits.astype(jnp.float32)], axis=0)
    ext = with_halo(stacked, (("along", 1), ("across", 2)), 6)
    grid_row = row_base - 6 + jnp.arange(rows + 12, dtype=jnp.int32)
    grid_col = col_base - 6 + jnp.arange(cols + 12, dtype=jnp.int32)
    inside_row = (grid_row >= 0) & (grid_row < total_rows)
    inside_col = (grid_col >= 0) & (grid_col < total_cols)
    present_wide = (inside_row[:, None] & inside_col[None, :]).astype(jnp.float32)
    present_ring = present_wide[3:-3, 3:-3]
    ring_bits = ext[4:6, 3:-3, 3:-3].astype(jnp.int32)
    words = [jnp.zeros((rows + 6, cols + 6), jnp.int32) for _ in range(2)]
    for index, (row_off, col_off) in enumerate(offsets):
        inside = present_wide[3 + row_off : 3 + row_off + rows + 6, 3 + col_off : 3 + col_off + cols + 6]
        words[index // 14] = words[index // 14] | jnp.left_shift(
            inside.astype(jnp.int32), index % 14
        )
    ring_bits = jnp.bitwise_and(ring_bits, jnp.stack(words))
    force = forces(ext[0:2], ring_bits, rows + 6, cols + 6)
    kept_sum, exist_sum = bond_counts(bond_bits, present_ring, rows, cols)
    damage = 1.0 - kept_sum / exist_sum
    ring_v = ext[2:4, 3:-3, 3:-3] + 10.0 * force
    ring_u = ext[0:2, 3:-3, 3:-3] + 0.05 * ring_v
    ring_u = jnp.where(present_ring[None] > 0.0, ring_u, 0.0)
    force = forces(ring_u, ring_bits[:, 3:-3, 3:-3], rows, cols)
    state_v = ring_v[:, 3:-3, 3:-3] + 10.0 * force
    state_u = ring_u[:, 3:-3, 3:-3] + 0.05 * state_v
    block_count = lax.axis_size("along")
    packed = jnp.concatenate(
        [panel_pos.reshape(1, -1), contact_list.astype(jnp.float32).reshape(1, -1)], axis=1
    )
    gathered = lax.all_to_all(
        jnp.broadcast_to(packed[None], (block_count,) + packed.shape), "along", 0, 0, tiled=True
    ).reshape(block_count, -1)
    gathered, state_u = lax.optimization_barrier((gathered, state_u))
    my_tile = lax.axis_index("along") * across_count + lax.axis_index("across")
    rows_x = (row_base + jnp.arange(rows, dtype=jnp.int32)).astype(jnp.float32)[:, None] + state_u[0]
    cols_x = (col_base + jnp.arange(cols, dtype=jnp.int32)).astype(jnp.float32)[None, :] + state_u[1]
    reach_row = 2.5 + jnp.max(jnp.abs(state_u[0]))
    reach_col = 2.5 + jnp.max(jnp.abs(state_u[1]))
    geometry = jnp.stack(
        [
            reach_row,
            reach_col,
            row_base.astype(jnp.float32),
            col_base.astype(jnp.float32),
            my_tile.astype(jnp.float32),
        ]
    )
    sums = contact_sums(geometry, gathered, rows_x, cols_x)
    partials = jnp.transpose(jnp.sum(sums, axis=-1), (0, 2, 1))
    spread = jnp.broadcast_to(
        partials.reshape(block_count, 1, 1, 2 * PAN_DEV),
        (block_count, across_count, 1, 2 * PAN_DEV),
    ).reshape(block_count * across_count, 1, 2 * PAN_DEV)
    arrived = lax.all_to_all(spread, ("along", "across"), 0, 0, tiled=True)
    panel_force = jnp.sum(arrived, axis=0).reshape(PAN_DEV, 2)
    return (state_u, state_v, damage, panel_force)


def solution(mesh):
    return jax.shard_map(
        body,
        mesh=mesh,
        in_specs=(
            P(None, "along", "across"),
            P(None, "along", "across"),
            P(None, "along", "across"),
            P("along", None),
            P("along", None),
        ),
        out_specs=(
            P(None, "along", "across"),
            P(None, "along", "across"),
            P("along", "across"),
            P("along", None),
        ),
        check_vma=False,
    )
```

```python
import jax
import jax.numpy as jnp
from jax import lax
from jax.experimental import pallas as pl
from jax.experimental.pallas import tpu as pltpu
from jax.sharding import PartitionSpec as P

PAN_DEV = 64


offsets = [(rr, cc) for rr in range(-3, 4) for cc in range(-3, 4) if 0 < rr * rr + cc * cc <= 9]


def contact_kernel(geo_ref, pos_ref, xr_ref, xc_ref, out_ref):
    out_ref[...] = jnp.zeros_like(out_ref)
    blocks, _, panels, _ = out_ref.shape
    rows, cols = xr_ref.shape
    row_tiles = rows // 8
    col_tiles = cols // 128
    reach_row, reach_col = geo_ref[0], geo_ref[1]
    row_base, col_base, my_tile = geo_ref[2], geo_ref[3], geo_ref[4]
    stride = pos_ref.shape[0] // blocks
    listing = stride - 2 * panels

    def window(centre, base, reach, size, group):
        local = centre - base
        low = jnp.clip((local - reach).astype(jnp.int32), 0, size)
        high = jnp.clip((local + reach).astype(jnp.int32) + 1, 0, size)
        first = low // group
        return first, jnp.maximum((high + group - 1) // group - first, 0)

    def tile_sums(centre_row, centre_col, row_group, col_group, accs):
        row = pl.multiple_of(row_group * 8, 8)
        col = pl.multiple_of(col_group * 128, 128)
        delta_row = centre_row - xr_ref[pl.ds(row, 8), pl.ds(col, 128)]
        delta_col = centre_col - xc_ref[pl.ds(row, 8), pl.ds(col, 128)]
        push = 0.5 * jnp.maximum(4.0 - delta_row * delta_row - delta_col * delta_col, 0.0)
        return (accs[0] + push * delta_row, accs[1] + push * delta_col)

    def store(block, j, accs):
        out_ref[block, 0, pl.ds(j, 1), :] = jnp.sum(accs[0], axis=0, keepdims=True)
        out_ref[block, 1, pl.ds(j, 1), :] = jnp.sum(accs[1], axis=0, keepdims=True)

    zero = jnp.zeros((8, 128), jnp.float32)

    def per_block_narrow(block):
        def per_panel(j, carry):
            centre_row = pos_ref[block * stride + 2 * j]
            centre_col = pos_ref[block * stride + 2 * j + 1]
            first_row, _ = window(centre_row, row_base, reach_row, rows, 8)
            first_col, _ = window(centre_col, col_base, reach_col, cols, 128)
            first_row = jnp.minimum(first_row, row_tiles - 2)
            first_col = jnp.minimum(first_col, col_tiles - 2)
            accs = (zero, zero)
            for r in range(2):
                for c in range(2):
                    accs = tile_sums(centre_row, centre_col, first_row + r, first_col + c, accs)
            store(block, j, accs)
            return carry

        lax.fori_loop(0, panels, per_panel, 0, unroll=16)

    def per_block_wide(block):
        def per_panel(j, carry):
            centre_row = pos_ref[block * stride + 2 * j]
            centre_col = pos_ref[block * stride + 2 * j + 1]
            first_row, row_groups = window(centre_row, row_base, reach_row, rows, 8)
            first_col, col_groups = window(centre_col, col_base, reach_col, cols, 128)

            def per_row(r, accs):
                def per_col(c, accs):
                    return tile_sums(centre_row, centre_col, first_row + r, first_col + c, accs)

                return lax.fori_loop(0, col_groups, per_col, accs)

            store(block, j, lax.fori_loop(0, row_groups, per_row, (zero, zero)))
            return carry

        lax.fori_loop(0, panels, per_panel, 0)

    narrow = (reach_row < 4.0) & (reach_col < 4.0)

    def per_block(block, carry):
        listed = pos_ref[block * stride + 2 * panels] == my_tile
        for slot in range(1, listing):
            listed = listed | (pos_ref[block * stride + 2 * panels + slot] == my_tile)

        @pl.when(listed & narrow)
        def _():
            per_block_narrow(block)

        @pl.when(listed & jnp.logical_not(narrow))
        def _():
            per_block_wide(block)

        return carry

    lax.fori_loop(0, blocks, per_block, 0)


def contact_sums(geometry, gathered, rows_x, cols_x):
    blocks = gathered.shape[0]
    smem = pl.BlockSpec(memory_space=pltpu.SMEM)
    vmem = pl.BlockSpec(memory_space=pltpu.VMEM)
    return pl.pallas_call(
        contact_kernel,
        out_shape=jax.ShapeDtypeStruct((blocks, 2, PAN_DEV, 128), jnp.float32),
        in_specs=[smem, smem, vmem, vmem],
        out_specs=vmem,
    )(geometry, gathered.reshape(-1), rows_x, cols_x)


def with_halo(block, sides, width):
    for axis, dim in sides:
        count = lax.axis_size(axis)
        forward = [(i, i + 1) for i in range(count - 1)]
        backward = [(target, source) for source, target in forward]
        narrow = dim == block.ndim - 1
        low = lax.slice_in_dim(block, block.shape[dim] - width, None, axis=dim)
        high = lax.slice_in_dim(block, 0, width, axis=dim)
        strip = low.shape
        if narrow:
            low, high = low.reshape(-1), high.reshape(-1)
        low = lax.ppermute(low, axis, forward).reshape(strip)
        high = lax.ppermute(high, axis, backward).reshape(strip)
        block = jnp.concatenate([low, block, high], axis=dim)
    return block


def bond_counts(bits, present_pad, rows, cols):
    kept_sum = jnp.zeros((rows, cols), jnp.float32)
    exist_sum = jnp.zeros((rows, cols), jnp.float32)
    for index, (row_off, col_off) in enumerate(offsets):
        present = present_pad[3 + row_off : 3 + row_off + rows, 3 + col_off : 3 + col_off + cols]
        flag = jnp.bitwise_and(jnp.right_shift(bits[index // 14], index % 14), 1).astype(
            jnp.float32
        )
        kept_sum = kept_sum + flag * present
        exist_sum = exist_sum + present
    return kept_sum, exist_sum


def forces(padded, bits, rows, cols):
    centre = padded[:, 3 : 3 + rows, 3 : 3 + cols]
    total_row = jnp.zeros((rows, cols), jnp.float32)
    total_col = jnp.zeros((rows, cols), jnp.float32)
    for index, (row_off, col_off) in enumerate(offsets):
        other = padded[:, 3 + row_off : 3 + row_off + rows, 3 + col_off : 3 + col_off + cols]
        keep = jnp.bitwise_and(jnp.right_shift(bits[index // 14], index % 14), 1).astype(
            jnp.float32
        )
        row_part = row_off + (other[0] - centre[0])
        col_part = col_off + (other[1] - centre[1])
        inv_length = lax.rsqrt(row_part * row_part + col_part * col_part)
        inv_rest = 1.0 / float((row_off * row_off + col_off * col_off) ** 0.5)
        coeff = keep * (inv_rest - inv_length)
        total_row = total_row + coeff * row_part
        total_col = total_col + coeff * col_part
    return jnp.stack([total_row, total_col])


def body(disp, velocity, bond_bits, panel_pos, contact_list):
    rows, cols = (disp.shape[1], disp.shape[2])
    along_count = lax.axis_size("along")
    across_count = lax.axis_size("across")
    total_rows = rows * along_count
    total_cols = cols * across_count
    row_base = lax.axis_index("along") * rows
    col_base = lax.axis_index("across") * cols
    stacked = jnp.concatenate([disp, velocity, bond_bits.astype(jnp.float32)], axis=0)
    ext = with_halo(stacked, (("along", 1), ("across", 2)), 6)
    grid_row = row_base - 6 + jnp.arange(rows + 12, dtype=jnp.int32)
    grid_col = col_base - 6 + jnp.arange(cols + 12, dtype=jnp.int32)
    inside_row = (grid_row >= 0) & (grid_row < total_rows)
    inside_col = (grid_col >= 0) & (grid_col < total_cols)
    present_wide = (inside_row[:, None] & inside_col[None, :]).astype(jnp.float32)
    present_ring = present_wide[3:-3, 3:-3]
    ring_bits = ext[4:6, 3:-3, 3:-3].astype(jnp.int32)
    words = [jnp.zeros((rows + 6, cols + 6), jnp.int32) for _ in range(2)]
    for index, (row_off, col_off) in enumerate(offsets):
        inside = present_wide[3 + row_off : 3 + row_off + rows + 6, 3 + col_off : 3 + col_off + cols + 6]
        words[index // 14] = words[index // 14] | jnp.left_shift(
            inside.astype(jnp.int32), index % 14
        )
    ring_bits = jnp.bitwise_and(ring_bits, jnp.stack(words))
    force = forces(ext[0:2], ring_bits, rows + 6, cols + 6)
    kept_sum, exist_sum = bond_counts(bond_bits, present_ring, rows, cols)
    damage = 1.0 - kept_sum / exist_sum
    ring_v = ext[2:4, 3:-3, 3:-3] + 10.0 * force
    ring_u = ext[0:2, 3:-3, 3:-3] + 0.05 * ring_v
    ring_u = jnp.where(present_ring[None] > 0.0, ring_u, 0.0)
    force = forces(ring_u, ring_bits[:, 3:-3, 3:-3], rows, cols)
    state_v = ring_v[:, 3:-3, 3:-3] + 10.0 * force
    state_u = ring_u[:, 3:-3, 3:-3] + 0.05 * state_v
    block_count = lax.axis_size("along")
    packed = jnp.concatenate(
        [panel_pos.reshape(1, -1), contact_list.astype(jnp.float32).reshape(1, -1)], axis=1
    )
    gathered = lax.all_to_all(
        jnp.broadcast_to(packed[None], (block_count,) + packed.shape), "along", 0, 0, tiled=True
    ).reshape(block_count, -1)
    gathered, state_u = lax.optimization_barrier((gathered, state_u))
    my_tile = lax.axis_index("along") * across_count + lax.axis_index("across")
    rows_x = (row_base + jnp.arange(rows, dtype=jnp.int32)).astype(jnp.float32)[:, None] + state_u[0]
    cols_x = (col_base + jnp.arange(cols, dtype=jnp.int32)).astype(jnp.float32)[None, :] + state_u[1]
    reach_row = 2.5 + jnp.max(jnp.abs(state_u[0]))
    reach_col = 2.5 + jnp.max(jnp.abs(state_u[1]))
    geometry = jnp.stack(
        [
            reach_row,
            reach_col,
            row_base.astype(jnp.float32),
            col_base.astype(jnp.float32),
            my_tile.astype(jnp.float32),
        ]
    )
    sums = contact_sums(geometry, gathered, rows_x, cols_x)
    partials = jnp.transpose(jnp.sum(sums, axis=-1), (0, 2, 1))
    spread = jnp.broadcast_to(
        partials.reshape(block_count, 1, 1, 2 * PAN_DEV),
        (block_count, across_count, 1, 2 * PAN_DEV),
    ).reshape(block_count * across_count, 1, 2 * PAN_DEV)
    arrived = lax.all_to_all(spread, ("along", "across"), 0, 0, tiled=True)
    panel_force = jnp.sum(arrived, axis=0).reshape(PAN_DEV, 2)
    return (state_u, state_v, damage, panel_force)


def solution(mesh):
    return jax.shard_map(
        body,
        mesh=mesh,
        in_specs=(
            P(None, "along", "across"),
            P(None, "along", "across"),
            P(None, "along", "across"),
            P("along", None),
            P("along", None),
        ),
        out_specs=(
            P(None, "along", "across"),
            P(None, "along", "across"),
            P("along", "across"),
            P("along", None),
        ),
        check_vma=False,
    )
```
